32 devices in a mesh: lat: 4 (over z), lon: 4 (over y, x), ens: 2 (over core).
Axes of the slice: x: 2, y: 2, z: 4, core: 2. Of those that a mesh axis runs over, the one named last changes fastest.
Arguments:
- field: bfloat16 [2048, 1920, 128], P(('ens', 'lat', 'lon')), parts along dimension 0, may hold values from -6 to 6
- w_first: bfloat16 [2, 128, 128], replicated, may hold values from -0.375 to 0.375
- b_first: float32 [2, 128], replicated, may hold values from -1.8 to 1.8
- w_second: bfloat16 [2, 128, 128], replicated, may hold values from -0.375 to 0.375
- b_second: float32 [2, 128], replicated, may hold values from -1.8 to 1.8
- conv_kernel: float32 [3, 3, 128], replicated, may hold values from -2 to 2
- mode_plan: int32 [16, 4], replicated, may hold values from -1 to 127, as said below
Outputs:
- block_output: bfloat16 [2048, 1920, 128], P(('ens', 'lat', 'lon')), parts along dimension 0
The draws below stay inside these ranges and needn't reach their ends.
There are 2 independent parts, one for each index of `ens`. The reference program is written for one: setup_inputs(seed, part) draws one part's arguments, and reference() takes and returns one part's arrays. A program takes and returns all parts, laid end to end along the dimension named above; an argument that names none is the same for every part. Nothing has to cross between parts.
Inputs may be any that keep to these rules, and one draw needn't show every extreme that they name: `mode_plan`: entry [o, s] is, for a listing device o = i * 4 + r, the local index of one tile of device i * 4 + s, or -1 for none; the indices that name one device's tiles are distinct; tiles that no entry names are dropped.
All inputs are finite; a program needn't handle non-finite values.
Results may differ from the reference program's by a relative error of at most 0.002.
Values may be sent and summed in bfloat16 or wider, within the bound.
No kernel may reach another device: no remote copies, remote signals or barrier semaphores. Data moves between devices by JAX's collectives and lax.ppermute only.
A program may use at most 960 MiB of HBM per device.

```python
import math
import jax
import jax.numpy as jnp
from jax import lax

H = 1024
W = 1920
C = 128
KH = 512
KW = 512
MB = 128
LAT_DEVS = 4
LON_DEVS = 4
TILES_DEV = 128
N_LAT = 4
N_LON = 4


def draw_mode_plan(key, part):
    device_total = LAT_DEVS * LON_DEVS
    key_list = jax.random.split(jax.random.fold_in(key, 11), device_total)

    def one_source(source_key):
        key_perm, key_slot = jax.random.split(source_key)
        shuffled = jax.random.permutation(key_perm, TILES_DEV).astype(jnp.int32)
        top_slot = jax.random.randint(key_slot, (), 0, LON_DEVS).astype(jnp.int32)
        where_top = jnp.argmax(shuffled == TILES_DEV - 1).astype(jnp.int32)
        positions = jnp.arange(TILES_DEV, dtype=jnp.int32)
        swapped = jnp.where(positions == top_slot, TILES_DEV - 1, jnp.where(positions == where_top, shuffled[top_slot], shuffled))
        return (swapped[:LON_DEVS], top_slot)
    chosen, top_slots = jax.vmap(one_source)(key_list)
    levels = jax.random.randint(jax.random.fold_in(key, 12), (device_total,), 1, 5).astype(jnp.int32)
    chance = jax.random.randint(jax.random.fold_in(key, 13), (device_total, LON_DEVS), 0, 4).astype(jnp.int32)
    sources = jnp.arange(device_total, dtype=jnp.int32)
    slots = jnp.arange(LON_DEVS, dtype=jnp.int32)[None, :]
    owner_row = (sources // LON_DEVS)[:, None] * LON_DEVS + slots
    retain = chance < levels[owner_row]
    retain = jnp.logical_or(retain, slots == top_slots[:, None])
    retain = jnp.logical_and(retain, slots != (top_slots[:, None] + 1) % LON_DEVS)
    by_source = jnp.where(retain, chosen, -1)
    result = jnp.transpose(by_source.reshape(LAT_DEVS, LON_DEVS, LON_DEVS), (0, 2, 1)).reshape(device_total, LON_DEVS)
    return result.astype(jnp.int32)


def level_of(key, shape, cuts, low, largest):
    factor_of, own = 1.0, jax.random.fold_in(key, 6)
    for position, parts in cuts:
        heights = jnp.exp(jax.random.uniform(jax.random.fold_in(own, position), (parts,), jnp.float32, low / len(cuts), largest / len(cuts)))
        factor_of = factor_of * jnp.repeat(heights, shape[position] // parts).reshape([-1 if axis == position else 1 for axis in range(len(shape))])
    return factor_of


def gaussian(own_key, shape, scale, reach, cuts=(), held_as=jnp.bfloat16):
    entries = jax.random.normal(own_key, shape, jnp.float32) * scale
    if len(cuts) > 0:
        entries = level_of(own_key, shape, cuts, -0.22, 0.18) * entries
    return jnp.clip(entries, min=-reach, max=reach).astype(held_as)


def setup_inputs(seed: int = 0, part: int = 0) -> dict:
    splits = jax.random.split(jax.random.key(seed), 8)
    part_splits = jax.random.split(jax.random.fold_in(splits[7], part), 8)
    field = gaussian(part_splits[0], (H, W, C), 1.0, 6.0, ((0, 16),))
    w_first = gaussian(splits[1], (2, C, C), (2 * C) ** -0.5, 0.375)
    b_first = gaussian(splits[2], (2, C), 0.3, 1.8, (), jnp.float32)
    w_second = gaussian(splits[3], (2, C, C), (2 * C) ** -0.5, 0.375)
    b_second = gaussian(splits[4], (2, C), 0.3, 1.8, (), jnp.float32)
    conv_kernel = gaussian(splits[5], (3, 3, C), 9 ** -0.5, 2.0, (), jnp.float32)
    mode_plan = draw_mode_plan(jax.random.fold_in(splits[7], 71), part)
    return dict(field=field, w_first=w_first, b_first=b_first, w_second=w_second, b_second=b_second, conv_kernel=conv_kernel, mode_plan=mode_plan)


shrink_level = 0.01

def lon_forward_matrix():
    columns = jnp.arange(W, dtype=jnp.int32)[:, None]
    orders = jnp.arange(KW, dtype=jnp.int32)[None, :]
    phases = columns * orders % W
    angles = phases.astype(jnp.float32) * (2.0 * math.pi / W)
    factor = 1.0 / math.sqrt(W)
    return (jnp.concatenate([jnp.cos(angles), -jnp.sin(angles)], axis=1) * factor).astype(jnp.bfloat16)

def lat_angles():
    freqs = jnp.arange(KH, dtype=jnp.int32) - KH // 2
    rowids = jnp.arange(H, dtype=jnp.int32)
    phases = jnp.mod(freqs[:, None] * rowids[None, :], H)
    return phases.astype(jnp.float32) * (2.0 * math.pi / H)

def lat_forward_matrix():
    angles = lat_angles()
    factor = 1.0 / math.sqrt(H)
    cosine = jnp.cos(angles) * factor
    sine = jnp.sin(angles) * factor
    upper = jnp.stack([cosine, sine], axis=1)
    lower = jnp.stack([-sine, cosine], axis=1)
    return jnp.concatenate([upper, lower], axis=0).astype(jnp.bfloat16)

def lat_inverse_matrix():
    angles = lat_angles()
    factor = 1.0 / math.sqrt(H)
    cosine = jnp.transpose(jnp.cos(angles)) * factor
    sine = jnp.transpose(jnp.sin(angles)) * factor
    real_rows = jnp.stack([cosine, -sine], axis=1)
    imag_rows = jnp.stack([sine, cosine], axis=1)
    return jnp.stack([real_rows, imag_rows], axis=0).astype(jnp.bfloat16)

def lon_inverse_matrix():
    orders = jnp.arange(KW, dtype=jnp.int32)[:, None]
    columns = jnp.arange(W, dtype=jnp.int32)[None, :]
    phases = orders * columns % W
    angles = phases.astype(jnp.float32) * (2.0 * math.pi / W)
    weights = jnp.where(orders == 0, 1.0, 2.0).astype(jnp.float32) / math.sqrt(W)
    return jnp.stack([weights * jnp.cos(angles), -weights * jnp.sin(angles)], axis=0).astype(jnp.bfloat16)

def complexify(weights):
    real_part = weights[0]
    imag_part = weights[1]
    top_rows = jnp.concatenate([real_part, imag_part], axis=1)
    low_rows = jnp.concatenate([-imag_part, real_part], axis=1)
    return jnp.concatenate([top_rows, low_rows], axis=0)

def spectral_mlp(modes, first_mat, first_bias, second_mat, second_bias):
    hidden = jnp.einsum('tmc,cd->tmd', modes.astype(jnp.float32), first_mat.astype(jnp.float32))
    hidden = jax.nn.relu(hidden + first_bias.reshape(-1)).astype(jnp.bfloat16)
    second_out = jnp.einsum('tmc,cd->tmd', hidden.astype(jnp.float32), second_mat.astype(jnp.float32))
    second_out = second_out + second_bias.reshape(-1)
    return second_out - jnp.clip(second_out, -shrink_level, shrink_level)

def layer_norm(values):
    values = values.astype(jnp.float32)
    average = lax.optimization_barrier(jnp.mean(values, axis=-1, keepdims=True))
    centred = values - average
    spread = lax.optimization_barrier(jnp.mean(centred * centred, axis=-1, keepdims=True))
    return (centred * lax.rsqrt(spread + 1e-05)).astype(jnp.bfloat16)

def reference(field, w_first, b_first, w_second, b_second, conv_kernel, mode_plan):
    devices = N_LAT * N_LON
    per_device = KW // devices
    tile_count = KH // MB * per_device
    row_block = math.gcd(H, 64)
    block_count = H // row_block
    lon_matrix = lon_forward_matrix().astype(jnp.float32)

    def forward_rows(portion):
        normed = layer_norm(portion)
        return jnp.einsum('hwc,wk->khc', normed.astype(jnp.float32), lon_matrix).astype(jnp.bfloat16)
    forward = lax.map(forward_rows, field.reshape(block_count, row_block, W, C))
    forward = jnp.transpose(forward, (1, 0, 2, 3)).reshape(2, KW, H, C)
    lat_matrix = lat_forward_matrix().astype(jnp.float32)
    grouped = jnp.transpose(forward.reshape(2, devices, per_device, H, C), (1, 0, 2, 3, 4))

    def lat_forward(portion):
        return jnp.einsum('pah,ajhc->jpc', lat_matrix, portion.astype(jnp.float32)).astype(jnp.bfloat16)
    spectrum = lax.map(lat_forward, grouped)
    tiles = spectrum.reshape(devices, per_device, 2, KH // MB, MB, C)
    tiles = jnp.transpose(tiles, (0, 1, 3, 4, 2, 5)).reshape(devices, tile_count, MB, 2 * C)
    plan_grid = mode_plan.reshape(N_LAT, N_LON, N_LON)
    matched = plan_grid[:, :, :, None] == jnp.arange(tile_count, dtype=jnp.int32)[None, None, None, :]
    retained = jnp.any(matched, axis=1).reshape(devices, tile_count)
    first_mat = complexify(w_first)
    second_mat = complexify(w_second)

    def filter_device(operands):
        device_tiles, device_kept = operands
        shrunk = spectral_mlp(device_tiles, first_mat, b_first, second_mat, b_second)
        return jnp.where(device_kept[:, None, None], shrunk, 0.0).astype(jnp.bfloat16)
    filtered = lax.map(filter_device, (tiles, retained))
    zspec = filtered.reshape(devices, per_device, KH // MB, MB, 2, C)
    zspec = jnp.transpose(zspec, (0, 1, 4, 2, 3, 5)).reshape(devices, per_device, 2, KH, C)
    inverse_lat = lat_inverse_matrix().astype(jnp.float32)

    def lat_inverse(portion):
        return jnp.einsum('ahbq,jbqc->ajhc', inverse_lat, portion.astype(jnp.float32)).astype(jnp.bfloat16)
    back = lax.map(lat_inverse, zspec)
    back = jnp.transpose(back, (1, 0, 2, 3, 4)).reshape(2, KW, H, C)
    rowwise = jnp.transpose(back.reshape(2, KW, block_count, row_block, C), (2, 0, 1, 3, 4))
    padded = jnp.pad(field, ((1, 1), (0, 0), (0, 0)))
    inverse_lon = lon_inverse_matrix().astype(jnp.float32)

    def finish(operands):
        row_index, portion = operands
        filtered_grid = jnp.einsum('akhc,akw->hwc', portion.astype(jnp.float32), inverse_lon).astype(jnp.bfloat16)
        extended = lax.dynamic_slice_in_dim(padded, row_index * row_block, row_block + 2, 0).astype(jnp.float32)
        stencil = jnp.zeros((row_block, W, C), jnp.float32)
        for row_off in range(3):
            for col_off in range(3):
                shifted = jnp.roll(extended[row_off:row_off + row_block], 1 - col_off, axis=1)
                stencil = stencil + conv_kernel[row_off, col_off] * shifted
        centre = extended[1:row_block + 1]
        return (centre + filtered_grid.astype(jnp.float32) + stencil).astype(jnp.bfloat16)
    result = lax.map(finish, (jnp.arange(block_count, dtype=jnp.int32), rowwise))
    return result.reshape(H, W, C)
```

```python
import math

import jax
import jax.numpy as jnp
from jax import lax
from jax.experimental import pallas as pl
from jax.experimental.pallas import tpu as pltpu
from jax.sharding import PartitionSpec as P

H = 1024
W = 1920
KH = 512
KW = 512
MB = 128


shrink_level = 0.01


def padded(block, sides, width):
    for axis, dim in sides:
        count = lax.axis_size(axis)
        forward = [(i, i + 1) for i in range(count - 1)]
        backward = [(target, source) for source, target in forward]
        low = lax.ppermute(
            lax.slice_in_dim(block, block.shape[dim] - width, None, axis=dim), axis, forward
        )
        high = lax.ppermute(lax.slice_in_dim(block, 0, width, axis=dim), axis, backward)
        block = jnp.concatenate([low, block, high], axis=dim)
    return block


def complexify(weights):
    real_part = weights[0]
    imag_part = weights[1]
    top_rows = jnp.concatenate([real_part, imag_part], axis=1)
    low_rows = jnp.concatenate([-imag_part, real_part], axis=1)
    return jnp.concatenate([top_rows, low_rows], axis=0)


def spectral_mlp(modes, first_mat, first_bias, second_mat, second_bias):
    hidden = jnp.einsum("tmc,cd->tmd", modes, first_mat, preferred_element_type=jnp.float32)
    hidden = jax.nn.relu(hidden + first_bias.reshape(-1)).astype(jnp.bfloat16)
    second_out = jnp.einsum("tmc,cd->tmd", hidden, second_mat, preferred_element_type=jnp.float32)
    second_out = second_out + second_bias.reshape(-1)
    return second_out - jnp.clip(second_out, -shrink_level, shrink_level)


def lon_angles(modes, width):
    columns = jnp.arange(width, dtype=jnp.int32)[:, None]
    phases = columns * modes[None, :] % width
    return phases.astype(jnp.float32) * (2.0 * math.pi / width)


def lat_trig(lat_modes, height):
    freqs = lat_modes - KH // 2
    rowids = jnp.arange(height, dtype=jnp.int32)
    phases = jnp.mod(freqs[..., None] * rowids, height)
    angles = phases.astype(jnp.float32) * (2.0 * math.pi / height)
    factor = 1.0 / math.sqrt(height)
    return jnp.cos(angles) * factor, jnp.sin(angles) * factor


def epilogue_kernel(taps_ref, above_ref, main_ref, below_ref, *refs):
    out_ref = refs[-1]
    block_rows, width, _ = main_ref.shape
    taps = [taps_ref[pl.ds(i, 1), :] for i in range(9)]

    def row(i):
        if i < 0:
            return above_ref[0].astype(jnp.float32)
        if i >= block_rows:
            return below_ref[0].astype(jnp.float32)
        return main_ref[i].astype(jnp.float32)

    for h in range(block_rows):
        acc = None
        for r in range(3):
            x = row(h + r - 1)
            left = pltpu.roll(x, 1, 0)
            right = pltpu.roll(x, width - 1, 0)
            term = taps[3 * r] * left + taps[3 * r + 1] * x + taps[3 * r + 2] * right
            acc = term if acc is None else acc + term
        if len(refs) == 3:
            grid_ref, lon_ref = refs[0], refs[1]
            wave = jnp.dot(lon_ref[...], grid_ref[h], preferred_element_type=jnp.float32)
            wave = wave.astype(jnp.bfloat16)
        else:
            wave = refs[0][h]
        out_ref[h] = ((row(h) + wave.astype(jnp.float32)) + acc).astype(jnp.bfloat16)


def epilogue(field, low, high, conv_kernel, wave_args):
    rows, width, channels = field.shape
    block_rows = math.gcd(rows, 4)
    count = rows // block_rows
    above = jnp.concatenate([low, field[block_rows - 1 : rows - 1 : block_rows]], axis=0)
    below = jnp.concatenate([field[block_rows::block_rows], high], axis=0)
    taps = conv_kernel.reshape(9, channels)
    row_spec = pl.BlockSpec((1, width, channels), lambda i: (i, 0, 0))
    main_spec = pl.BlockSpec((block_rows, width, channels), lambda i: (i, 0, 0))
    if len(wave_args) == 2:
        grid_rows, lon_inv = wave_args
        n = grid_rows.shape[1]
        wave_specs = [
            pl.BlockSpec((block_rows, n, channels), lambda i: (i, 0, 0)),
            pl.BlockSpec((width, n), lambda i: (0, 0)),
        ]
    else:
        wave_specs = [main_spec]
    return pl.pallas_call(
        epilogue_kernel,
        grid=(count,),
        in_specs=[pl.BlockSpec((9, channels), lambda i: (0, 0)), row_spec, main_spec, row_spec]
        + wave_specs,
        out_specs=main_spec,
        out_shape=jax.ShapeDtypeStruct((rows, width, channels), jnp.bfloat16),
        compiler_params=pltpu.CompilerParams(dimension_semantics=("arbitrary",)),
    )(taps, above, field, below, *wave_args)


def on_device(field, w_first, b_first, w_second, b_second, conv_kernel, mode_plan):
    rows, width, channels = field.shape
    lat_count = lax.axis_size("lat")
    lon_count = lax.axis_size("lon")
    devs = lat_count * lon_count
    per_device = KW // devs
    blocks = KH // MB
    slots = mode_plan.shape[0] // lat_count
    height = rows * devs
    me = lax.axis_index("lat") * lon_count + lax.axis_index("lon")

    plan = mode_plan.reshape(lat_count, slots, lon_count).transpose(0, 2, 1).reshape(devs, slots)
    valid = plan >= 0
    tile = jnp.maximum(plan, 0)
    local_mode = tile // blocks
    lat_block = tile % blocks
    modes = jnp.arange(devs, dtype=jnp.int32)[:, None] * per_device + local_mode

    values = field.astype(jnp.float32)
    average = jnp.mean(values, axis=-1, keepdims=True)
    centred = values - average
    spread = jnp.mean(centred * centred, axis=-1, keepdims=True)
    normed = (centred * lax.rsqrt(spread + 1e-05)).astype(jnp.bfloat16)
    angles = lon_angles(modes.reshape(-1), width)
    factor = 1.0 / math.sqrt(width)
    lon_sub = (jnp.stack([jnp.cos(angles), -jnp.sin(angles)], axis=-1) * factor).astype(jnp.bfloat16)
    forward = jnp.einsum("hwc,wna->nahc", normed, lon_sub, preferred_element_type=jnp.float32)
    forward = forward.astype(jnp.bfloat16).reshape(devs, slots, 2, rows, channels)
    pencil = lax.all_to_all(forward, ("lat", "lon"), split_axis=0, concat_axis=0, tiled=True)

    my_block = lax.dynamic_index_in_dim(lat_block, me, 0, keepdims=False)
    my_valid = lax.dynamic_index_in_dim(valid, me, 0, keepdims=False)
    my_mode = lax.dynamic_index_in_dim(local_mode, me, 0, keepdims=False)
    lat_modes = my_block[:, None] * MB + jnp.arange(MB, dtype=jnp.int32)[None, :]
    cosine, sine = lat_trig(lat_modes, height)
    lat_fwd = jnp.stack(
        [jnp.stack([cosine, sine], axis=2), jnp.stack([-sine, cosine], axis=2)], axis=1
    ).astype(jnp.bfloat16)
    lat_fwd = lat_fwd.reshape(slots, 2, MB, 2, devs, rows)
    spectrum = jnp.einsum(
        "joqasr,sjarc->jqoc", lat_fwd, pencil, preferred_element_type=jnp.float32
    )
    tiles = spectrum.astype(jnp.bfloat16).reshape(slots, MB, 2 * channels)

    first_mat = complexify(w_first)
    second_mat = complexify(w_second)
    shrunk = spectral_mlp(tiles, first_mat, b_first, second_mat, b_second)
    filtered = jnp.where(my_valid[:, None, None], shrunk, 0.0).astype(jnp.bfloat16)
    filtered = filtered.reshape(slots, MB, 2, channels)

    lat_inv = jnp.stack(
        [jnp.stack([cosine, -sine], axis=1), jnp.stack([sine, cosine], axis=1)], axis=1
    ).astype(jnp.bfloat16)
    lat_inv = lat_inv.reshape(slots, 2, 2, MB, devs, rows)
    partial = jnp.einsum(
        "jabqsr,jqbc->sjarc", lat_inv, filtered, preferred_element_type=jnp.float32
    )
    same = (my_mode[:, None] == my_mode[None, :]) & my_valid[None, :]
    earlier = jnp.tril(jnp.ones((slots, slots), jnp.bool_), -1)
    first = my_valid & ~jnp.any(same & earlier, axis=1)
    merge = (same & first[:, None]).astype(jnp.float32)
    combined = jnp.einsum(
        "jk,skarc->sjarc", merge, partial, precision=lax.Precision.HIGHEST,
        preferred_element_type=jnp.float32,
    )
    inverse = combined.astype(jnp.bfloat16)
    rowwise = lax.all_to_all(inverse, ("lat", "lon"), split_axis=0, concat_axis=0, tiled=True)

    inv_angles = lon_angles(modes.reshape(-1), width)
    weights = jnp.where(modes.reshape(-1) == 0, 1.0, 2.0).astype(jnp.float32) / math.sqrt(width)
    lon_inv = jnp.stack(
        [weights * jnp.cos(inv_angles), -weights * jnp.sin(inv_angles)], axis=-1
    ).astype(jnp.bfloat16)
    lon_inv = lon_inv.reshape(width, devs * slots * 2)
    grid_rows = jnp.transpose(rowwise, (3, 0, 1, 2, 4)).reshape(rows, devs * slots * 2, channels)
    if devs * slots * 2 <= 512:
        wave_args = (grid_rows, lon_inv)
    else:
        wave = jnp.einsum("rnc,wn->rwc", grid_rows, lon_inv, preferred_element_type=jnp.float32)
        wave_args = (wave.astype(jnp.bfloat16),)

    count = devs
    forward_pairs = [(i, i + 1) for i in range(count - 1)]
    backward_pairs = [(t, s) for s, t in forward_pairs]
    low = lax.ppermute(field[rows - 1 :], ("lat", "lon"), forward_pairs)
    high = lax.ppermute(field[:1], ("lat", "lon"), backward_pairs)
    return epilogue(field, low, high, conv_kernel, wave_args)


def solution(mesh):
    placed = (P(("ens", "lat", "lon"), None, None), P(), P(), P(), P(), P(), P())
    return jax.shard_map(
        on_device,
        mesh=mesh,
        in_specs=placed,
        out_specs=P(("ens", "lat", "lon"), None, None),
        check_vma=False,
    )
```

```python
import math

import jax
import jax.numpy as jnp
from jax import lax
from jax.experimental import pallas as pl
from jax.experimental.pallas import tpu as pltpu
from jax.sharding import PartitionSpec as P

H = 1024
W = 1920
KH = 512
KW = 512
MB = 128


shrink_level = 0.01


def complexify(weights):
    real_part = weights[0]
    imag_part = weights[1]
    top_rows = jnp.concatenate([real_part, imag_part], axis=1)
    low_rows = jnp.concatenate([-imag_part, real_part], axis=1)
    return jnp.concatenate([top_rows, low_rows], axis=0)


def spectral_mlp(modes, first_mat, first_bias, second_mat, second_bias):
    hidden = jnp.einsum("tmc,cd->tmd", modes, first_mat, preferred_element_type=jnp.float32)
    hidden = jax.nn.relu(hidden + first_bias.reshape(-1)).astype(jnp.bfloat16)
    second_out = jnp.einsum("tmc,cd->tmd", hidden, second_mat, preferred_element_type=jnp.float32)
    second_out = second_out + second_bias.reshape(-1)
    return second_out - jnp.clip(second_out, -shrink_level, shrink_level)


def lon_angles(modes, width):
    columns = jnp.arange(width, dtype=jnp.int32)[:, None]
    phases = columns * modes[None, :] % width
    return phases.astype(jnp.float32) * (2.0 * math.pi / width)


def lat_trig(lat_modes, height):
    freqs = lat_modes - KH // 2
    rowids = jnp.arange(height, dtype=jnp.int32)
    phases = jnp.mod(freqs[..., None] * rowids, height)
    angles = phases.astype(jnp.float32) * (2.0 * math.pi / height)
    factor = 1.0 / math.sqrt(height)
    return jnp.cos(angles) * factor, jnp.sin(angles) * factor


def forward_kernel(field_ref, lon_ref, out_ref):
    block_rows, _, channels = field_ref.shape
    lon = lon_ref[...]
    for h in range(block_rows):
        x = field_ref[h].astype(jnp.float32)
        average = jnp.sum(x, axis=1, keepdims=True) * (1.0 / channels)
        centred = x - average
        spread = jnp.sum(centred * centred, axis=1, keepdims=True) * (1.0 / channels)
        normed = (centred * lax.rsqrt(spread + 1e-05)).astype(jnp.bfloat16)
        out_ref[h] = jnp.dot(lon, normed, preferred_element_type=jnp.float32).astype(jnp.bfloat16)


def forward_rows(field, lon_t):
    rows, width, channels = field.shape
    n = lon_t.shape[0]
    block_rows = math.gcd(rows, 4)
    return pl.pallas_call(
        forward_kernel,
        grid=(rows // block_rows,),
        in_specs=[
            pl.BlockSpec((block_rows, width, channels), lambda i: (i, 0, 0)),
            pl.BlockSpec((n, width), lambda i: (0, 0)),
        ],
        out_specs=pl.BlockSpec((block_rows, n, channels), lambda i: (i, 0, 0)),
        out_shape=jax.ShapeDtypeStruct((rows, n, channels), jnp.bfloat16),
        compiler_params=pltpu.CompilerParams(dimension_semantics=("arbitrary",)),
    )(field, lon_t)


def epilogue_kernel(taps_ref, above_ref, main_ref, below_ref, *refs):
    out_ref = refs[-1]
    block_rows, width, _ = main_ref.shape
    taps = [taps_ref[pl.ds(i, 1), :] for i in range(9)]

    def row(i):
        if i < 0:
            return above_ref[0].astype(jnp.float32)
        if i >= block_rows:
            return below_ref[0].astype(jnp.float32)
        return main_ref[i].astype(jnp.float32)

    for h in range(block_rows):
        acc = None
        for r in range(3):
            x = row(h + r - 1)
            left = pltpu.roll(x, 1, 0)
            right = pltpu.roll(x, width - 1, 0)
            term = taps[3 * r] * left + taps[3 * r + 1] * x + taps[3 * r + 2] * right
            acc = term if acc is None else acc + term
        if len(refs) == 3:
            grid_ref, lon_ref = refs[0], refs[1]
            wave = jnp.dot(lon_ref[...], grid_ref[h], preferred_element_type=jnp.float32)
            wave = wave.astype(jnp.bfloat16)
        else:
            wave = refs[0][h]
        out_ref[h] = ((row(h) + wave.astype(jnp.float32)) + acc).astype(jnp.bfloat16)


def epilogue(field, low, high, conv_kernel, wave_args):
    rows, width, channels = field.shape
    block_rows = math.gcd(rows, 4)
    count = rows // block_rows
    above = jnp.concatenate([low, field[block_rows - 1 : rows - 1 : block_rows]], axis=0)
    below = jnp.concatenate([field[block_rows::block_rows], high], axis=0)
    taps = conv_kernel.reshape(9, channels)
    row_spec = pl.BlockSpec((1, width, channels), lambda i: (i, 0, 0))
    main_spec = pl.BlockSpec((block_rows, width, channels), lambda i: (i, 0, 0))
    if len(wave_args) == 2:
        grid_rows, lon_inv = wave_args
        n = grid_rows.shape[1]
        wave_specs = [
            pl.BlockSpec((block_rows, n, channels), lambda i: (i, 0, 0)),
            pl.BlockSpec((width, n), lambda i: (0, 0)),
        ]
    else:
        wave_specs = [main_spec]
    return pl.pallas_call(
        epilogue_kernel,
        grid=(count,),
        in_specs=[pl.BlockSpec((9, channels), lambda i: (0, 0)), row_spec, main_spec, row_spec]
        + wave_specs,
        out_specs=main_spec,
        out_shape=jax.ShapeDtypeStruct((rows, width, channels), jnp.bfloat16),
        compiler_params=pltpu.CompilerParams(dimension_semantics=("arbitrary",)),
    )(taps, above, field, below, *wave_args)


def on_device(field, w_first, b_first, w_second, b_second, conv_kernel, mode_plan):
    rows, width, channels = field.shape
    lat_count = lax.axis_size("lat")
    lon_count = lax.axis_size("lon")
    devs = lat_count * lon_count
    per_device = KW // devs
    blocks = KH // MB
    slots = mode_plan.shape[0] // lat_count
    height = rows * devs
    me = lax.axis_index("lat") * lon_count + lax.axis_index("lon")

    plan = mode_plan.reshape(lat_count, slots, lon_count).transpose(0, 2, 1).reshape(devs, slots)
    valid = plan >= 0
    tile = jnp.maximum(plan, 0)
    local_mode = tile // blocks
    lat_block = tile % blocks
    modes = jnp.arange(devs, dtype=jnp.int32)[:, None] * per_device + local_mode

    angles = lon_angles(modes.reshape(-1), width)
    factor = 1.0 / math.sqrt(width)
    lon_sub = (jnp.stack([jnp.cos(angles), -jnp.sin(angles)], axis=-1) * factor).astype(jnp.bfloat16)
    if devs * slots * 2 <= 512:
        lon_t = jnp.transpose(lon_sub, (1, 2, 0)).reshape(devs * slots * 2, width)
        forward = forward_rows(field, lon_t).reshape(rows, devs, slots, 2, channels)
        forward = jnp.transpose(forward, (1, 2, 3, 0, 4))
    else:
        values = field.astype(jnp.float32)
        average = jnp.mean(values, axis=-1, keepdims=True)
        centred = values - average
        spread = jnp.mean(centred * centred, axis=-1, keepdims=True)
        normed = (centred * lax.rsqrt(spread + 1e-05)).astype(jnp.bfloat16)
        forward = jnp.einsum("hwc,wna->nahc", normed, lon_sub, preferred_element_type=jnp.float32)
        forward = forward.astype(jnp.bfloat16).reshape(devs, slots, 2, rows, channels)
    pencil = lax.all_to_all(forward, ("lat", "lon"), split_axis=0, concat_axis=0, tiled=True)

    my_block = lax.dynamic_index_in_dim(lat_block, me, 0, keepdims=False)
    my_valid = lax.dynamic_index_in_dim(valid, me, 0, keepdims=False)
    my_mode = lax.dynamic_index_in_dim(local_mode, me, 0, keepdims=False)
    lat_modes = my_block[:, None] * MB + jnp.arange(MB, dtype=jnp.int32)[None, :]
    cosine, sine = lat_trig(lat_modes, height)
    lat_fwd = jnp.stack(
        [jnp.stack([cosine, sine], axis=2), jnp.stack([-sine, cosine], axis=2)], axis=1
    ).astype(jnp.bfloat16)
    lat_fwd = lat_fwd.reshape(slots, 2, MB, 2, devs, rows)
    spectrum = jnp.einsum(
        "joqasr,sjarc->jqoc", lat_fwd, pencil, preferred_element_type=jnp.float32
    )
    tiles = spectrum.astype(jnp.bfloat16).reshape(slots, MB, 2 * channels)

    first_mat = complexify(w_first)
    second_mat = complexify(w_second)
    shrunk = spectral_mlp(tiles, first_mat, b_first, second_mat, b_second)
    filtered = jnp.where(my_valid[:, None, None], shrunk, 0.0).astype(jnp.bfloat16)
    filtered = filtered.reshape(slots, MB, 2, channels)

    lat_inv = jnp.stack(
        [jnp.stack([cosine, -sine], axis=1), jnp.stack([sine, cosine], axis=1)], axis=1
    ).astype(jnp.bfloat16)
    lat_inv = lat_inv.reshape(slots, 2, 2, MB, devs, rows)
    partial = jnp.einsum(
        "jabqsr,jqbc->sjarc", lat_inv, filtered, preferred_element_type=jnp.float32
    )
    same = (my_mode[:, None] == my_mode[None, :]) & my_valid[None, :]
    earlier = jnp.tril(jnp.ones((slots, slots), jnp.bool_), -1)
    first = my_valid & ~jnp.any(same & earlier, axis=1)
    merge = (same & first[:, None]).astype(jnp.float32)
    combined = jnp.einsum(
        "jk,skarc->sjarc", merge, partial, precision=lax.Precision.HIGHEST,
        preferred_element_type=jnp.float32,
    )
    inverse = combined.astype(jnp.bfloat16)
    rowwise = lax.all_to_all(inverse, ("lat", "lon"), split_axis=0, concat_axis=0, tiled=True)

    inv_angles = lon_angles(modes.reshape(-1), width)
    weights = jnp.where(modes.reshape(-1) == 0, 1.0, 2.0).astype(jnp.float32) / math.sqrt(width)
    lon_inv = jnp.stack(
        [weights * jnp.cos(inv_angles), -weights * jnp.sin(inv_angles)], axis=-1
    ).astype(jnp.bfloat16)
    lon_inv = lon_inv.reshape(width, devs * slots * 2)
    grid_rows = jnp.transpose(rowwise, (3, 0, 1, 2, 4)).reshape(rows, devs * slots * 2, channels)
    if devs * slots * 2 <= 512:
        wave_args = (grid_rows, lon_inv)
    else:
        wave = jnp.einsum("rnc,wn->rwc", grid_rows, lon_inv, preferred_element_type=jnp.float32)
        wave_args = (wave.astype(jnp.bfloat16),)

    count = devs
    forward_pairs = [(i, i + 1) for i in range(count - 1)]
    backward_pairs = [(t, s) for s, t in forward_pairs]
    low = lax.ppermute(field[rows - 1 :], ("lat", "lon"), forward_pairs)
    high = lax.ppermute(field[:1], ("lat", "lon"), backward_pairs)
    return epilogue(field, low, high, conv_kernel, wave_args)


def solution(mesh):
    placed = (P(("ens", "lat", "lon"), None, None), P(), P(), P(), P(), P(), P())
    return jax.shard_map(
        on_device,
        mesh=mesh,
        in_specs=placed,
        out_specs=P(("ens", "lat", "lon"), None, None),
        check_vma=False,
    )
```

```python
import math

import jax
import jax.numpy as jnp
from jax import lax
from jax.experimental import pallas as pl
from jax.experimental.pallas import tpu as pltpu
from jax.sharding import PartitionSpec as P

H = 1024
W = 1920
KH = 512
KW = 512
MB = 128


shrink_level = 0.01


def complexify(weights):
    real_part = weights[0]
    imag_part = weights[1]
    top_rows = jnp.concatenate([real_part, imag_part], axis=1)
    low_rows = jnp.concatenate([-imag_part, real_part], axis=1)
    return jnp.concatenate([top_rows, low_rows], axis=0)


def spectral_mlp(modes, first_mat, first_bias, second_mat, second_bias):
    hidden = jnp.einsum("tmc,cd->tmd", modes, first_mat, preferred_element_type=jnp.float32)
    hidden = jax.nn.relu(hidden + first_bias.reshape(-1)).astype(jnp.bfloat16)
    second_out = jnp.einsum("tmc,cd->tmd", hidden, second_mat, preferred_element_type=jnp.float32)
    second_out = second_out + second_bias.reshape(-1)
    return second_out - jnp.clip(second_out, -shrink_level, shrink_level)


def lon_angles(modes, width):
    columns = jnp.arange(width, dtype=jnp.int32)[:, None]
    phases = columns * modes[None, :] % width
    return phases.astype(jnp.float32) * (2.0 * math.pi / width)


def lat_trig(lat_modes, height):
    freqs = lat_modes - KH // 2
    rowids = jnp.arange(height, dtype=jnp.int32)
    phases = jnp.mod(freqs[..., None] * rowids, height)
    angles = phases.astype(jnp.float32) * (2.0 * math.pi / height)
    factor = 1.0 / math.sqrt(height)
    return jnp.cos(angles) * factor, jnp.sin(angles) * factor


def forward_kernel(field_ref, lon_ref, out_ref):
    block_rows, _, channels = field_ref.shape
    lon = lon_ref[...]
    for h in range(block_rows):
        x = field_ref[h].astype(jnp.float32)
        average = jnp.sum(x, axis=1, keepdims=True) * (1.0 / channels)
        centred = x - average
        spread = jnp.sum(centred * centred, axis=1, keepdims=True) * (1.0 / channels)
        normed = (centred * lax.rsqrt(spread + 1e-05)).astype(jnp.bfloat16)
        out_ref[h] = jnp.dot(lon, normed, preferred_element_type=jnp.float32).astype(jnp.bfloat16)


def forward_rows(field, lon_t):
    rows, width, channels = field.shape
    n = lon_t.shape[0]
    block_rows = math.gcd(rows, 4)
    return pl.pallas_call(
        forward_kernel,
        grid=(rows // block_rows,),
        in_specs=[
            pl.BlockSpec((block_rows, width, channels), lambda i: (i, 0, 0)),
            pl.BlockSpec((n, width), lambda i: (0, 0)),
        ],
        out_specs=pl.BlockSpec((block_rows, n, channels), lambda i: (i, 0, 0)),
        out_shape=jax.ShapeDtypeStruct((rows, n, channels), jnp.bfloat16),
        compiler_params=pltpu.CompilerParams(dimension_semantics=("arbitrary",)),
    )(field, lon_t)


def epilogue_kernel(taps_ref, low_ref, high_ref, above_ref, main_ref, below_ref, *refs):
    out_ref = refs[-1]
    block_rows, width, _ = main_ref.shape
    step = pl.program_id(0)
    taps = [taps_ref[pl.ds(i, 1), :] for i in range(9)]
    first_row = jnp.where(step == 0, low_ref[0], above_ref[0]).astype(jnp.float32)
    last_row = jnp.where(step == pl.num_programs(0) - 1, high_ref[0], below_ref[0])
    last_row = last_row.astype(jnp.float32)

    def row(i):
        if i < 0:
            return first_row
        if i >= block_rows:
            return last_row
        return main_ref[i].astype(jnp.float32)

    for h in range(block_rows):
        xs = [row(h - 1), row(h), row(h + 1)]
        cols = [taps[s] * xs[0] + taps[3 + s] * xs[1] + taps[6 + s] * xs[2] for s in range(3)]
        stencil = pltpu.roll(cols[0], 1, 0) + cols[1] + pltpu.roll(cols[2], width - 1, 0)
        if len(refs) == 3:
            grid_ref, lon_ref = refs[0], refs[1]
            wave = jnp.dot(lon_ref[...], grid_ref[h], preferred_element_type=jnp.float32)
            wave = wave.astype(jnp.bfloat16)
        else:
            wave = refs[0][h]
        out_ref[h] = ((xs[1] + wave.astype(jnp.float32)) + stencil).astype(jnp.bfloat16)


def epilogue(field, low, high, conv_kernel, wave_args):
    rows, width, channels = field.shape
    block_rows = math.gcd(rows, 4)
    count = rows // block_rows
    taps = conv_kernel.reshape(9, channels)
    halo_spec = pl.BlockSpec((1, width, channels), lambda i: (0, 0, 0))
    above_spec = pl.BlockSpec(
        (1, width, channels), lambda i: (jnp.maximum(i * block_rows - 1, 0), 0, 0)
    )
    below_spec = pl.BlockSpec(
        (1, width, channels), lambda i: (jnp.minimum((i + 1) * block_rows, rows - 1), 0, 0)
    )
    main_spec = pl.BlockSpec((block_rows, width, channels), lambda i: (i, 0, 0))
    if len(wave_args) == 2:
        grid_rows, lon_inv = wave_args
        n = grid_rows.shape[1]
        wave_specs = [
            pl.BlockSpec((block_rows, n, channels), lambda i: (i, 0, 0)),
            pl.BlockSpec((width, n), lambda i: (0, 0)),
        ]
    else:
        wave_specs = [main_spec]
    return pl.pallas_call(
        epilogue_kernel,
        grid=(count,),
        in_specs=[pl.BlockSpec((9, channels), lambda i: (0, 0)), halo_spec, halo_spec]
        + [above_spec, main_spec, below_spec]
        + wave_specs,
        out_specs=main_spec,
        out_shape=jax.ShapeDtypeStruct((rows, width, channels), jnp.bfloat16),
        compiler_params=pltpu.CompilerParams(dimension_semantics=("arbitrary",)),
    )(taps, low, high, field, field, field, *wave_args)


def on_device(field, w_first, b_first, w_second, b_second, conv_kernel, mode_plan):
    rows, width, channels = field.shape
    lat_count = lax.axis_size("lat")
    lon_count = lax.axis_size("lon")
    devs = lat_count * lon_count
    per_device = KW // devs
    blocks = KH // MB
    slots = mode_plan.shape[0] // lat_count
    height = rows * devs
    me = lax.axis_index("lat") * lon_count + lax.axis_index("lon")

    plan = mode_plan.reshape(lat_count, slots, lon_count).transpose(0, 2, 1).reshape(devs, slots)
    valid = plan >= 0
    tile = jnp.maximum(plan, 0)
    local_mode = tile // blocks
    lat_block = tile % blocks
    modes = jnp.arange(devs, dtype=jnp.int32)[:, None] * per_device + local_mode

    angles = lon_angles(modes.reshape(-1), width)
    factor = 1.0 / math.sqrt(width)
    lon_sub = (jnp.stack([jnp.cos(angles), -jnp.sin(angles)], axis=-1) * factor).astype(jnp.bfloat16)
    if devs * slots * 2 <= 512:
        lon_t = jnp.transpose(lon_sub, (1, 2, 0)).reshape(devs * slots * 2, width)
        forward = forward_rows(field, lon_t).reshape(rows, devs, slots, 2, channels)
        forward = jnp.transpose(forward, (1, 2, 3, 0, 4))
    else:
        values = field.astype(jnp.float32)
        average = jnp.mean(values, axis=-1, keepdims=True)
        centred = values - average
        spread = jnp.mean(centred * centred, axis=-1, keepdims=True)
        normed = (centred * lax.rsqrt(spread + 1e-05)).astype(jnp.bfloat16)
        forward = jnp.einsum("hwc,wna->nahc", normed, lon_sub, preferred_element_type=jnp.float32)
        forward = forward.astype(jnp.bfloat16).reshape(devs, slots, 2, rows, channels)
    pencil = lax.all_to_all(forward, ("lat", "lon"), split_axis=0, concat_axis=0, tiled=True)

    my_block = lax.dynamic_index_in_dim(lat_block, me, 0, keepdims=False)
    my_valid = lax.dynamic_index_in_dim(valid, me, 0, keepdims=False)
    my_mode = lax.dynamic_index_in_dim(local_mode, me, 0, keepdims=False)
    lat_modes = my_block[:, None] * MB + jnp.arange(MB, dtype=jnp.int32)[None, :]
    cosine, sine = lat_trig(lat_modes, height)
    lat_fwd = jnp.stack(
        [jnp.stack([cosine, sine], axis=2), jnp.stack([-sine, cosine], axis=2)], axis=1
    ).astype(jnp.bfloat16)
    lat_fwd = lat_fwd.reshape(slots, 2, MB, 2, devs, rows)
    spectrum = jnp.einsum(
        "joqasr,sjarc->jqoc", lat_fwd, pencil, preferred_element_type=jnp.float32
    )
    tiles = spectrum.astype(jnp.bfloat16).reshape(slots, MB, 2 * channels)

    first_mat = complexify(w_first)
    second_mat = complexify(w_second)
    shrunk = spectral_mlp(tiles, first_mat, b_first, second_mat, b_second)
    filtered = jnp.where(my_valid[:, None, None], shrunk, 0.0).astype(jnp.bfloat16)
    filtered = filtered.reshape(slots, MB, 2, channels)

    lat_inv = jnp.stack(
        [jnp.stack([cosine, -sine], axis=1), jnp.stack([sine, cosine], axis=1)], axis=1
    ).astype(jnp.bfloat16)
    lat_inv = lat_inv.reshape(slots, 2, 2, MB, devs, rows)
    partial = jnp.einsum(
        "jabqsr,jqbc->sjarc", lat_inv, filtered, preferred_element_type=jnp.float32
    )
    same = (my_mode[:, None] == my_mode[None, :]) & my_valid[None, :]
    earlier = jnp.tril(jnp.ones((slots, slots), jnp.bool_), -1)
    first = my_valid & ~jnp.any(same & earlier, axis=1)
    merge = (same & first[:, None]).astype(jnp.float32)
    combined = jnp.einsum(
        "jk,skarc->sjarc", merge, partial, precision=lax.Precision.HIGHEST,
        preferred_element_type=jnp.float32,
    )
    inverse = combined.astype(jnp.bfloat16)
    rowwise = lax.all_to_all(inverse, ("lat", "lon"), split_axis=0, concat_axis=0, tiled=True)

    inv_angles = lon_angles(modes.reshape(-1), width)
    weights = jnp.where(modes.reshape(-1) == 0, 1.0, 2.0).astype(jnp.float32) / math.sqrt(width)
    lon_inv = jnp.stack(
        [weights * jnp.cos(inv_angles), -weights * jnp.sin(inv_angles)], axis=-1
    ).astype(jnp.bfloat16)
    lon_inv = lon_inv.reshape(width, devs * slots * 2)
    grid_rows = jnp.transpose(rowwise, (3, 0, 1, 2, 4)).reshape(rows, devs * slots * 2, channels)
    if devs * slots * 2 <= 512:
        wave_args = (grid_rows, lon_inv)
    else:
        wave = jnp.einsum("rnc,wn->rwc", grid_rows, lon_inv, preferred_element_type=jnp.float32)
        wave_args = (wave.astype(jnp.bfloat16),)

    count = devs
    forward_pairs = [(i, i + 1) for i in range(count - 1)]
    backward_pairs = [(t, s) for s, t in forward_pairs]
    low = lax.ppermute(field[rows - 1 :], ("lat", "lon"), forward_pairs)
    high = lax.ppermute(field[:1], ("lat", "lon"), backward_pairs)
    return epilogue(field, low, high, conv_kernel, wave_args)


def solution(mesh):
    placed = (P(("ens", "lat", "lon"), None, None), P(), P(), P(), P(), P(), P())
    return jax.shard_map(
        on_device,
        mesh=mesh,
        in_specs=placed,
        out_specs=P(("ens", "lat", "lon"), None, None),
        check_vma=False,
    )
```

```python
import math

import jax
import jax.numpy as jnp
from jax import lax
from jax.experimental import pallas as pl
from jax.experimental.pallas import tpu as pltpu
from jax.sharding import PartitionSpec as P

H = 1024
W = 1920
KH = 512
KW = 512
MB = 128


shrink_level = 0.01


def complexify(weights):
    real_part = weights[0]
    imag_part = weights[1]
    top_rows = jnp.concatenate([real_part, imag_part], axis=1)
    low_rows = jnp.concatenate([-imag_part, real_part], axis=1)
    return jnp.concatenate([top_rows, low_rows], axis=0)


def spectral_mlp(modes, first_mat, first_bias, second_mat, second_bias):
    hidden = jnp.einsum("tmc,cd->tmd", modes, first_mat, preferred_element_type=jnp.float32)
    hidden = jax.nn.relu(hidden + first_bias.reshape(-1)).astype(jnp.bfloat16)
    second_out = jnp.einsum("tmc,cd->tmd", hidden, second_mat, preferred_element_type=jnp.float32)
    second_out = second_out + second_bias.reshape(-1)
    return second_out - jnp.clip(second_out, -shrink_level, shrink_level)


def lon_angles(modes, width):
    columns = jnp.arange(width, dtype=jnp.int32)[:, None]
    phases = columns * modes[None, :] % width
    return phases.astype(jnp.float32) * (2.0 * math.pi / width)


def lat_trig(lat_modes, height):
    freqs = lat_modes - KH // 2
    rowids = jnp.arange(height, dtype=jnp.int32)
    phases = jnp.mod(freqs[..., None] * rowids, height)
    angles = phases.astype(jnp.float32) * (2.0 * math.pi / height)
    factor = 1.0 / math.sqrt(height)
    return jnp.cos(angles) * factor, jnp.sin(angles) * factor


def forward_kernel(field_ref, lon_ref, out_ref):
    block_rows, _, channels = field_ref.shape
    lon = lon_ref[...]
    for h in range(block_rows):
        x = field_ref[h].astype(jnp.float32)
        average = jnp.sum(x, axis=1, keepdims=True) * (1.0 / channels)
        centred = x - average
        spread = jnp.sum(centred * centred, axis=1, keepdims=True) * (1.0 / channels)
        normed = (centred * lax.rsqrt(spread + 1e-05)).astype(jnp.bfloat16)
        out_ref[h] = jnp.dot(lon, normed, preferred_element_type=jnp.float32).astype(jnp.bfloat16)


def forward_rows(field, lon_t, start, count):
    _, width, channels = field.shape
    n = lon_t.shape[0]
    block_rows = math.gcd(count, 4)
    offset = start // block_rows
    return pl.pallas_call(
        forward_kernel,
        grid=(count // block_rows,),
        in_specs=[
            pl.BlockSpec((block_rows, width, channels), lambda i: (i + offset, 0, 0)),
            pl.BlockSpec((n, width), lambda i: (0, 0)),
        ],
        out_specs=pl.BlockSpec((block_rows, n, channels), lambda i: (i, 0, 0)),
        out_shape=jax.ShapeDtypeStruct((count, n, channels), jnp.bfloat16),
        compiler_params=pltpu.CompilerParams(dimension_semantics=("arbitrary",)),
    )(field, lon_t)


def make_epilogue_kernel(in_wave, first_block, last_block):
    def kernel(taps_ref, low_ref, high_ref, above_ref, main_ref, below_ref, *refs):
        out_ref = refs[-1]
        block_rows, width, _ = main_ref.shape
        step = pl.program_id(0) + first_block
        taps = [taps_ref[pl.ds(i, 1), :] for i in range(9)]
        first_row = jnp.where(step == 0, low_ref[0], above_ref[0]).astype(jnp.float32)
        last_row = jnp.where(step == last_block, high_ref[0], below_ref[0])
        last_row = last_row.astype(jnp.float32)

        def row(i):
            if i < 0:
                return first_row
            if i >= block_rows:
                return last_row
            return main_ref[i].astype(jnp.float32)

        for h in range(block_rows):
            xs = [row(h - 1), row(h), row(h + 1)]
            cols = [taps[s] * xs[0] + taps[3 + s] * xs[1] + taps[6 + s] * xs[2] for s in range(3)]
            stencil = pltpu.roll(cols[0], 1, 0) + cols[1] + pltpu.roll(cols[2], width - 1, 0)
            if in_wave:
                grid_ref, lon_ref = refs[0], refs[1]
                wave = jnp.dot(lon_ref[...], grid_ref[h], preferred_element_type=jnp.float32)
                wave = wave.astype(jnp.bfloat16)
            else:
                wave = refs[0][h]
            out_ref[h] = ((xs[1] + wave.astype(jnp.float32)) + stencil).astype(jnp.bfloat16)

    return kernel


def epilogue(field, low, high, conv_kernel, wave_args, start, count, prior):
    rows, width, channels = field.shape
    block_rows = math.gcd(count, 4)
    offset = start // block_rows
    taps = conv_kernel.reshape(9, channels)
    halo_spec = pl.BlockSpec((1, width, channels), lambda i: (0, 0, 0))
    above_spec = pl.BlockSpec(
        (1, width, channels), lambda i: (jnp.maximum((i + offset) * block_rows - 1, 0), 0, 0)
    )
    below_spec = pl.BlockSpec(
        (1, width, channels),
        lambda i: (jnp.minimum((i + offset + 1) * block_rows, rows - 1), 0, 0),
    )
    main_spec = pl.BlockSpec((block_rows, width, channels), lambda i: (i + offset, 0, 0))
    in_wave = len(wave_args) == 2
    if in_wave:
        grid_rows, lon_inv = wave_args
        n = grid_rows.shape[1]
        wave_specs = [
            pl.BlockSpec((block_rows, n, channels), lambda i: (i, 0, 0)),
            pl.BlockSpec((width, n), lambda i: (0, 0)),
        ]
    else:
        wave_specs = [pl.BlockSpec((block_rows, width, channels), lambda i: (i, 0, 0))]
    operands = [taps, low, high, field, field, field, *wave_args]
    specs = [pl.BlockSpec((9, channels), lambda i: (0, 0)), halo_spec, halo_spec]
    specs += [above_spec, main_spec, below_spec] + wave_specs
    aliases = {}
    if prior is not None:
        aliases = {len(operands): 0}
        operands.append(prior)
        specs.append(pl.BlockSpec(memory_space=pl.ANY))
    kernel = make_epilogue_kernel(in_wave, offset, rows // block_rows - 1)
    return pl.pallas_call(
        kernel,
        grid=(count // block_rows,),
        in_specs=specs,
        out_specs=main_spec,
        out_shape=jax.ShapeDtypeStruct((rows, width, channels), jnp.bfloat16),
        input_output_aliases=aliases,
        compiler_params=pltpu.CompilerParams(dimension_semantics=("arbitrary",)),
    )(*operands)


def on_device(field, w_first, b_first, w_second, b_second, conv_kernel, mode_plan):
    rows, width, channels = field.shape
    lat_count = lax.axis_size("lat")
    lon_count = lax.axis_size("lon")
    devs = lat_count * lon_count
    per_device = KW // devs
    blocks = KH // MB
    slots = mode_plan.shape[0] // lat_count
    height = rows * devs
    me = lax.axis_index("lat") * lon_count + lax.axis_index("lon")
    n = devs * slots * 2
    chunks = 2 if rows % 8 == 0 else 1
    part = rows // chunks

    plan = mode_plan.reshape(lat_count, slots, lon_count).transpose(0, 2, 1).reshape(devs, slots)
    valid = plan >= 0
    tile = jnp.maximum(plan, 0)
    local_mode = tile // blocks
    lat_block = tile % blocks
    modes = jnp.arange(devs, dtype=jnp.int32)[:, None] * per_device + local_mode

    angles = lon_angles(modes.reshape(-1), width)
    factor = 1.0 / math.sqrt(width)
    lon_sub = (jnp.stack([jnp.cos(angles), -jnp.sin(angles)], axis=-1) * factor).astype(jnp.bfloat16)
    pencils = []
    if n <= 512:
        lon_t = jnp.transpose(lon_sub, (1, 2, 0)).reshape(n, width)
        for c in range(chunks):
            forward = forward_rows(field, lon_t, c * part, part)
            forward = forward.reshape(part, devs, slots, 2, channels)
            forward = jnp.transpose(forward, (1, 2, 3, 0, 4))
            pencils.append(
                lax.all_to_all(forward, ("lat", "lon"), split_axis=0, concat_axis=0, tiled=True)
            )
    else:
        values = field.astype(jnp.float32)
        average = jnp.mean(values, axis=-1, keepdims=True)
        centred = values - average
        spread = jnp.mean(centred * centred, axis=-1, keepdims=True)
        normed = (centred * lax.rsqrt(spread + 1e-05)).astype(jnp.bfloat16)
        forward = jnp.einsum("hwc,wna->nahc", normed, lon_sub, preferred_element_type=jnp.float32)
        forward = forward.astype(jnp.bfloat16).reshape(devs, slots, 2, rows, channels)
        chunks, part = 1, rows
        pencils.append(
            lax.all_to_all(forward, ("lat", "lon"), split_axis=0, concat_axis=0, tiled=True)
        )

    my_block = lax.dynamic_index_in_dim(lat_block, me, 0, keepdims=False)
    my_valid = lax.dynamic_index_in_dim(valid, me, 0, keepdims=False)
    my_mode = lax.dynamic_index_in_dim(local_mode, me, 0, keepdims=False)
    lat_modes = my_block[:, None] * MB + jnp.arange(MB, dtype=jnp.int32)[None, :]
    cosine, sine = lat_trig(lat_modes, height)
    lat_fwd = jnp.stack(
        [jnp.stack([cosine, sine], axis=2), jnp.stack([-sine, cosine], axis=2)], axis=1
    ).astype(jnp.bfloat16)
    lat_fwd = lat_fwd.reshape(slots, 2, MB, 2, devs, rows)
    spectrum = None
    for c in range(chunks):
        term = jnp.einsum(
            "joqasr,sjarc->jqoc",
            lat_fwd[..., c * part : (c + 1) * part],
            pencils[c],
            preferred_element_type=jnp.float32,
        )
        spectrum = term if spectrum is None else spectrum + term
    tiles = spectrum.astype(jnp.bfloat16).reshape(slots, MB, 2 * channels)

    first_mat = complexify(w_first)
    second_mat = complexify(w_second)
    shrunk = spectral_mlp(tiles, first_mat, b_first, second_mat, b_second)
    filtered = jnp.where(my_valid[:, None, None], shrunk, 0.0).astype(jnp.bfloat16)
    filtered = filtered.reshape(slots, MB, 2, channels)

    lat_inv = jnp.stack(
        [jnp.stack([cosine, -sine], axis=1), jnp.stack([sine, cosine], axis=1)], axis=1
    ).astype(jnp.bfloat16)
    lat_inv = lat_inv.reshape(slots, 2, 2, MB, devs, rows)
    same = (my_mode[:, None] == my_mode[None, :]) & my_valid[None, :]
    earlier = jnp.tril(jnp.ones((slots, slots), jnp.bool_), -1)
    first = my_valid & ~jnp.any(same & earlier, axis=1)
    merge = (same & first[:, None]).astype(jnp.float32)

    inv_angles = lon_angles(modes.reshape(-1), width)
    weights = jnp.where(modes.reshape(-1) == 0, 1.0, 2.0).astype(jnp.float32) / math.sqrt(width)
    lon_inv = jnp.stack(
        [weights * jnp.cos(inv_angles), -weights * jnp.sin(inv_angles)], axis=-1
    ).astype(jnp.bfloat16)
    lon_inv = lon_inv.reshape(width, n)

    forward_pairs = [(i, i + 1) for i in range(devs - 1)]
    backward_pairs = [(t, s) for s, t in forward_pairs]
    low = lax.ppermute(field[rows - 1 :], ("lat", "lon"), forward_pairs)
    high = lax.ppermute(field[:1], ("lat", "lon"), backward_pairs)

    partial = jnp.einsum(
        "jabqsr,jqbc->sjarc", lat_inv, filtered, preferred_element_type=jnp.float32
    )
    combined = jnp.einsum(
        "jk,skarc->sjarc", merge, partial, precision=lax.Precision.HIGHEST,
        preferred_element_type=jnp.float32,
    )
    inverse = combined.astype(jnp.bfloat16)
    rowwise = lax.all_to_all(inverse, ("lat", "lon"), split_axis=0, concat_axis=0, tiled=True)
    grid_rows = jnp.transpose(rowwise, (3, 0, 1, 2, 4)).reshape(rows, n, channels)
    if n <= 512:
        wave_args = (grid_rows, lon_inv)
    else:
        wave = jnp.einsum("rnc,wn->rwc", grid_rows, lon_inv, preferred_element_type=jnp.float32)
        wave_args = (wave.astype(jnp.bfloat16),)
    return epilogue(field, low, high, conv_kernel, wave_args, 0, rows, None)


def solution(mesh):
    placed = (P(("ens", "lat", "lon"), None, None), P(), P(), P(), P(), P(), P())
    return jax.shard_map(
        on_device,
        mesh=mesh,
        in_specs=placed,
        out_specs=P(("ens", "lat", "lon"), None, None),
        check_vma=False,
    )
```

```python
import math

import jax
import jax.numpy as jnp
from jax import lax
from jax.experimental import pallas as pl
from jax.experimental.pallas import tpu as pltpu
from jax.sharding import PartitionSpec as P

H = 1024
W = 1920
KH = 512
KW = 512
MB = 128


shrink_level = 0.01


def complexify(weights):
    real_part = weights[0]
    imag_part = weights[1]
    top_rows = jnp.concatenate([real_part, imag_part], axis=1)
    low_rows = jnp.concatenate([-imag_part, real_part], axis=1)
    return jnp.concatenate([top_rows, low_rows], axis=0)


def spectral_mlp(modes, first_mat, first_bias, second_mat, second_bias):
    hidden = jnp.einsum("tmc,cd->tmd", modes, first_mat, preferred_element_type=jnp.float32)
    hidden = jax.nn.relu(hidden + first_bias.reshape(-1)).astype(jnp.bfloat16)
    second_out = jnp.einsum("tmc,cd->tmd", hidden, second_mat, preferred_element_type=jnp.float32)
    second_out = second_out + second_bias.reshape(-1)
    return second_out - jnp.clip(second_out, -shrink_level, shrink_level)


def lon_angles(modes, width):
    columns = jnp.arange(width, dtype=jnp.int32)[:, None]
    phases = columns * modes[None, :] % width
    return phases.astype(jnp.float32) * (2.0 * math.pi / width)


def lat_trig(lat_modes, height):
    freqs = lat_modes - KH // 2
    rowids = jnp.arange(height, dtype=jnp.int32)
    phases = jnp.mod(freqs[..., None] * rowids, height)
    angles = phases.astype(jnp.float32) * (2.0 * math.pi / height)
    factor = 1.0 / math.sqrt(height)
    return jnp.cos(angles) * factor, jnp.sin(angles) * factor


def forward_kernel(field_ref, lon_ref, out_ref):
    block_rows, _, channels = field_ref.shape
    lon = lon_ref[...]
    ones = jnp.ones((channels, channels), jnp.bfloat16)
    for h in range(block_rows):
        raw = field_ref[h]
        total = jnp.dot(raw, ones, preferred_element_type=jnp.float32)
        average = total * (1.0 / channels)
        centred = raw.astype(jnp.float32) - average
        square = centred * centred
        high = square.astype(jnp.bfloat16)
        low = (square - high.astype(jnp.float32)).astype(jnp.bfloat16)
        spread = jnp.dot(high, ones, preferred_element_type=jnp.float32)
        spread = (spread + jnp.dot(low, ones, preferred_element_type=jnp.float32)) * (1.0 / channels)
        normed = (centred * lax.rsqrt(spread + 1e-05)).astype(jnp.bfloat16)
        out_ref[h] = jnp.dot(lon, normed, preferred_element_type=jnp.float32).astype(jnp.bfloat16)


def forward_rows(field, lon_t, start, count):
    _, width, channels = field.shape
    n = lon_t.shape[0]
    block_rows = math.gcd(count, 4)
    offset = start // block_rows
    return pl.pallas_call(
        forward_kernel,
        grid=(count // block_rows,),
        in_specs=[
            pl.BlockSpec((block_rows, width, channels), lambda i: (i + offset, 0, 0)),
            pl.BlockSpec((n, width), lambda i: (0, 0)),
        ],
        out_specs=pl.BlockSpec((block_rows, n, channels), lambda i: (i, 0, 0)),
        out_shape=jax.ShapeDtypeStruct((count, n, channels), jnp.bfloat16),
        compiler_params=pltpu.CompilerParams(dimension_semantics=("arbitrary",)),
    )(field, lon_t)


def make_epilogue_kernel(in_wave, first_block, last_block):
    def kernel(taps_ref, low_ref, high_ref, above_ref, main_ref, below_ref, *refs):
        out_ref = refs[-1]
        block_rows, width, _ = main_ref.shape
        step = pl.program_id(0) + first_block
        taps = [taps_ref[pl.ds(i, 1), :] for i in range(9)]
        first_row = jnp.where(step == 0, low_ref[0], above_ref[0]).astype(jnp.float32)
        last_row = jnp.where(step == last_block, high_ref[0], below_ref[0])
        last_row = last_row.astype(jnp.float32)

        def row(i):
            if i < 0:
                return first_row
            if i >= block_rows:
                return last_row
            return main_ref[i].astype(jnp.float32)

        for h in range(block_rows):
            xs = [row(h - 1), row(h), row(h + 1)]
            cols = [taps[s] * xs[0] + taps[3 + s] * xs[1] + taps[6 + s] * xs[2] for s in range(3)]
            stencil = pltpu.roll(cols[0], 1, 0) + cols[1] + pltpu.roll(cols[2], width - 1, 0)
            if in_wave:
                grid_ref, lon_ref = refs[0], refs[1]
                wave = jnp.dot(lon_ref[...], grid_ref[h], preferred_element_type=jnp.float32)
            else:
                wave = refs[0][h].astype(jnp.float32)
            out_ref[h] = ((xs[1] + wave) + stencil).astype(jnp.bfloat16)

    return kernel


def epilogue(field, low, high, conv_kernel, wave_args, start, count, prior):
    rows, width, channels = field.shape
    block_rows = math.gcd(count, 4)
    offset = start // block_rows
    taps = conv_kernel.reshape(9, channels)
    halo_spec = pl.BlockSpec((1, width, channels), lambda i: (0, 0, 0))
    above_spec = pl.BlockSpec(
        (1, width, channels), lambda i: (jnp.maximum((i + offset) * block_rows - 1, 0), 0, 0)
    )
    below_spec = pl.BlockSpec(
        (1, width, channels),
        lambda i: (jnp.minimum((i + offset + 1) * block_rows, rows - 1), 0, 0),
    )
    main_spec = pl.BlockSpec((block_rows, width, channels), lambda i: (i + offset, 0, 0))
    in_wave = len(wave_args) == 2
    if in_wave:
        grid_rows, lon_inv = wave_args
        n = grid_rows.shape[1]
        wave_specs = [
            pl.BlockSpec((block_rows, n, channels), lambda i: (i, 0, 0)),
            pl.BlockSpec((width, n), lambda i: (0, 0)),
        ]
    else:
        wave_specs = [pl.BlockSpec((block_rows, width, channels), lambda i: (i, 0, 0))]
    operands = [taps, low, high, field, field, field, *wave_args]
    specs = [pl.BlockSpec((9, channels), lambda i: (0, 0)), halo_spec, halo_spec]
    specs += [above_spec, main_spec, below_spec] + wave_specs
    aliases = {}
    if prior is not None:
        aliases = {len(operands): 0}
        operands.append(prior)
        specs.append(pl.BlockSpec(memory_space=pl.ANY))
    kernel = make_epilogue_kernel(in_wave, offset, rows // block_rows - 1)
    return pl.pallas_call(
        kernel,
        grid=(count // block_rows,),
        in_specs=specs,
        out_specs=main_spec,
        out_shape=jax.ShapeDtypeStruct((rows, width, channels), jnp.bfloat16),
        input_output_aliases=aliases,
        compiler_params=pltpu.CompilerParams(dimension_semantics=("arbitrary",)),
    )(*operands)


def on_device(field, w_first, b_first, w_second, b_second, conv_kernel, mode_plan):
    rows, width, channels = field.shape
    lat_count = lax.axis_size("lat")
    lon_count = lax.axis_size("lon")
    devs = lat_count * lon_count
    per_device = KW // devs
    blocks = KH // MB
    slots = mode_plan.shape[0] // lat_count
    height = rows * devs
    me = lax.axis_index("lat") * lon_count + lax.axis_index("lon")
    n = devs * slots * 2
    chunks = 2 if rows % 8 == 0 else 1
    part = rows // chunks

    plan = mode_plan.reshape(lat_count, slots, lon_count).transpose(0, 2, 1).reshape(devs, slots)
    valid = plan >= 0
    tile = jnp.maximum(plan, 0)
    local_mode = tile // blocks
    lat_block = tile % blocks
    modes = jnp.arange(devs, dtype=jnp.int32)[:, None] * per_device + local_mode

    angles = lon_angles(modes.reshape(-1), width)
    factor = 1.0 / math.sqrt(width)
    lon_sub = (jnp.stack([jnp.cos(angles), -jnp.sin(angles)], axis=-1) * factor).astype(jnp.bfloat16)
    pencils = []
    if n <= 512:
        lon_t = jnp.transpose(lon_sub, (1, 2, 0)).reshape(n, width)
        for c in range(chunks):
            forward = forward_rows(field, lon_t, c * part, part)
            forward = forward.reshape(part, devs, slots, 2, channels)
            forward = jnp.transpose(forward, (1, 2, 3, 0, 4))
            pencils.append(
                lax.all_to_all(forward, ("lat", "lon"), split_axis=0, concat_axis=0, tiled=True)
            )
    else:
        values = field.astype(jnp.float32)
        average = jnp.mean(values, axis=-1, keepdims=True)
        centred = values - average
        spread = jnp.mean(centred * centred, axis=-1, keepdims=True)
        normed = (centred * lax.rsqrt(spread + 1e-05)).astype(jnp.bfloat16)
        forward = jnp.einsum("hwc,wna->nahc", normed, lon_sub, preferred_element_type=jnp.float32)
        forward = forward.astype(jnp.bfloat16).reshape(devs, slots, 2, rows, channels)
        chunks, part = 1, rows
        pencils.append(
            lax.all_to_all(forward, ("lat", "lon"), split_axis=0, concat_axis=0, tiled=True)
        )

    my_block = lax.dynamic_index_in_dim(lat_block, me, 0, keepdims=False)
    my_valid = lax.dynamic_index_in_dim(valid, me, 0, keepdims=False)
    my_mode = lax.dynamic_index_in_dim(local_mode, me, 0, keepdims=False)
    lat_modes = my_block[:, None] * MB + jnp.arange(MB, dtype=jnp.int32)[None, :]
    cosine, sine = lat_trig(lat_modes, height)
    lat_fwd = jnp.stack(
        [jnp.stack([cosine, sine], axis=2), jnp.stack([-sine, cosine], axis=2)], axis=1
    ).astype(jnp.bfloat16)
    lat_fwd = lat_fwd.reshape(slots, 2, MB, 2, devs, rows)
    spectrum = None
    for c in range(chunks):
        term = jnp.einsum(
            "joqasr,sjarc->jqoc",
            lat_fwd[..., c * part : (c + 1) * part],
            pencils[c],
            preferred_element_type=jnp.float32,
        )
        spectrum = term if spectrum is None else spectrum + term
    tiles = spectrum.astype(jnp.bfloat16).reshape(slots, MB, 2 * channels)

    first_mat = complexify(w_first)
    second_mat = complexify(w_second)
    shrunk = spectral_mlp(tiles, first_mat, b_first, second_mat, b_second)
    filtered = jnp.where(my_valid[:, None, None], shrunk, 0.0).astype(jnp.bfloat16)
    filtered = filtered.reshape(slots, MB, 2, channels)

    lat_inv = jnp.stack(
        [jnp.stack([cosine, -sine], axis=1), jnp.stack([sine, cosine], axis=1)], axis=1
    ).astype(jnp.bfloat16)
    lat_inv = lat_inv.reshape(slots, 2, 2, MB, devs, rows)
    same = (my_mode[:, None] == my_mode[None, :]) & my_valid[None, :]
    earlier = jnp.tril(jnp.ones((slots, slots), jnp.bool_), -1)
    first = my_valid & ~jnp.any(same & earlier, axis=1)
    merge = (same & first[:, None]).astype(jnp.float32)

    inv_angles = lon_angles(modes.reshape(-1), width)
    weights = jnp.where(modes.reshape(-1) == 0, 1.0, 2.0).astype(jnp.float32) / math.sqrt(width)
    lon_inv = jnp.stack(
        [weights * jnp.cos(inv_angles), -weights * jnp.sin(inv_angles)], axis=-1
    ).astype(jnp.bfloat16)
    lon_inv = lon_inv.reshape(width, n)

    forward_pairs = [(i, i + 1) for i in range(devs - 1)]
    backward_pairs = [(t, s) for s, t in forward_pairs]
    low = lax.ppermute(field[rows - 1 :], ("lat", "lon"), forward_pairs)
    high = lax.ppermute(field[:1], ("lat", "lon"), backward_pairs)

    partial = jnp.einsum(
        "jabqsr,jqbc->sjarc", lat_inv, filtered, preferred_element_type=jnp.float32
    )
    combined = jnp.einsum(
        "jk,skarc->sjarc", merge, partial, precision=lax.Precision.HIGHEST,
        preferred_element_type=jnp.float32,
    )
    inverse = combined.astype(jnp.bfloat16)
    rowwise = lax.all_to_all(inverse, ("lat", "lon"), split_axis=0, concat_axis=0, tiled=True)
    grid_rows = jnp.transpose(rowwise, (3, 0, 1, 2, 4)).reshape(rows, n, channels)
    if n <= 512:
        wave_args = (grid_rows, lon_inv)
    else:
        wave = jnp.einsum("rnc,wn->rwc", grid_rows, lon_inv, preferred_element_type=jnp.float32)
        wave_args = (wave.astype(jnp.bfloat16),)
    return epilogue(field, low, high, conv_kernel, wave_args, 0, rows, None)


def solution(mesh):
    placed = (P(("ens", "lat", "lon"), None, None), P(), P(), P(), P(), P(), P())
    return jax.shard_map(
        on_device,
        mesh=mesh,
        in_specs=placed,
        out_specs=P(("ens", "lat", "lon"), None, None),
        check_vma=False,
    )
```

```python
import math

import jax
import jax.numpy as jnp
from jax import lax
from jax.experimental import pallas as pl
from jax.experimental.pallas import tpu as pltpu
from jax.sharding import PartitionSpec as P

H = 1024
W = 1920
KH = 512
KW = 512
MB = 128


shrink_level = 0.01


def complexify(weights):
    real_part = weights[0]
    imag_part = weights[1]
    top_rows = jnp.concatenate([real_part, imag_part], axis=1)
    low_rows = jnp.concatenate([-imag_part, real_part], axis=1)
    return jnp.concatenate([top_rows, low_rows], axis=0)


def spectral_mlp(modes, first_mat, first_bias, second_mat, second_bias):
    hidden = jnp.einsum("tmc,cd->tmd", modes, first_mat, preferred_element_type=jnp.float32)
    hidden = jax.nn.relu(hidden + first_bias.reshape(-1)).astype(jnp.bfloat16)
    second_out = jnp.einsum("tmc,cd->tmd", hidden, second_mat, preferred_element_type=jnp.float32)
    second_out = second_out + second_bias.reshape(-1)
    return second_out - jnp.clip(second_out, -shrink_level, shrink_level)


def lon_angles(modes, width):
    columns = jnp.arange(width, dtype=jnp.int32)[:, None]
    phases = columns * modes[None, :] % width
    return phases.astype(jnp.float32) * (2.0 * math.pi / width)


def lat_trig(lat_modes, height):
    freqs = lat_modes - KH // 2
    rowids = jnp.arange(height, dtype=jnp.int32)
    phases = jnp.mod(freqs[..., None] * rowids, height)
    angles = phases.astype(jnp.float32) * (2.0 * math.pi / height)
    factor = 1.0 / math.sqrt(height)
    return jnp.cos(angles) * factor, jnp.sin(angles) * factor


def forward_kernel(field_ref, lon_ref, out_ref):
    block_rows, _, channels = field_ref.shape
    lon = lon_ref[...]
    for h in range(block_rows):
        x = field_ref[h].astype(jnp.float32)
        average = jnp.sum(x, axis=1, keepdims=True) * (1.0 / channels)
        centred = x - average
        spread = jnp.sum(centred * centred, axis=1, keepdims=True) * (1.0 / channels)
        normed = (centred * lax.rsqrt(spread + 1e-05)).astype(jnp.bfloat16)
        out_ref[h] = jnp.dot(lon, normed, preferred_element_type=jnp.float32).astype(jnp.bfloat16)


def forward_rows(field, lon_t, start, count):
    _, width, channels = field.shape
    n = lon_t.shape[0]
    block_rows = math.gcd(count, 4)
    offset = start // block_rows
    return pl.pallas_call(
        forward_kernel,
        grid=(count // block_rows,),
        in_specs=[
            pl.BlockSpec((block_rows, width, channels), lambda i: (i + offset, 0, 0)),
            pl.BlockSpec((n, width), lambda i: (0, 0)),
        ],
        out_specs=pl.BlockSpec((block_rows, n, channels), lambda i: (i, 0, 0)),
        out_shape=jax.ShapeDtypeStruct((count, n, channels), jnp.bfloat16),
        compiler_params=pltpu.CompilerParams(dimension_semantics=("arbitrary",)),
    )(field, lon_t)


def make_epilogue_kernel(in_wave, first_block, last_block):
    def kernel(taps_ref, low_ref, high_ref, above_ref, main_ref, below_ref, *refs):
        out_ref = refs[-1]
        block_rows, width, _ = main_ref.shape
        step = pl.program_id(0) + first_block
        taps = [taps_ref[pl.ds(i, 1), :] for i in range(9)]
        first_row = jnp.where(step == 0, low_ref[0], above_ref[0]).astype(jnp.float32)
        last_row = jnp.where(step == last_block, high_ref[0], below_ref[0])
        last_row = last_row.astype(jnp.float32)

        def row(i):
            if i < 0:
                return first_row
            if i >= block_rows:
                return last_row
            return main_ref[i].astype(jnp.float32)

        for h in range(block_rows):
            xs = [row(h - 1), row(h), row(h + 1)]
            cols = [taps[s] * xs[0] + taps[3 + s] * xs[1] + taps[6 + s] * xs[2] for s in range(3)]
            stencil = pltpu.roll(cols[0], 1, 0) + cols[1] + pltpu.roll(cols[2], width - 1, 0)
            if in_wave:
                grid_ref, lon_ref = refs[0], refs[1]
                wave = jnp.dot(lon_ref[...], grid_ref[h], preferred_element_type=jnp.float32)
            else:
                wave = refs[0][h].astype(jnp.float32)
            out_ref[h] = ((xs[1] + wave) + stencil).astype(jnp.bfloat16)

    return kernel


def epilogue(field, low, high, conv_kernel, wave_args, start, count, prior):
    rows, width, channels = field.shape
    block_rows = math.gcd(count, 8)
    offset = start // block_rows
    taps = conv_kernel.reshape(9, channels)
    halo_spec = pl.BlockSpec((1, width, channels), lambda i: (0, 0, 0))
    above_spec = pl.BlockSpec(
        (1, width, channels), lambda i: (jnp.maximum((i + offset) * block_rows - 1, 0), 0, 0)
    )
    below_spec = pl.BlockSpec(
        (1, width, channels),
        lambda i: (jnp.minimum((i + offset + 1) * block_rows, rows - 1), 0, 0),
    )
    main_spec = pl.BlockSpec((block_rows, width, channels), lambda i: (i + offset, 0, 0))
    in_wave = len(wave_args) == 2
    if in_wave:
        grid_rows, lon_inv = wave_args
        n = grid_rows.shape[1]
        wave_specs = [
            pl.BlockSpec((block_rows, n, channels), lambda i: (i, 0, 0)),
            pl.BlockSpec((width, n), lambda i: (0, 0)),
        ]
    else:
        wave_specs = [pl.BlockSpec((block_rows, width, channels), lambda i: (i, 0, 0))]
    operands = [taps, low, high, field, field, field, *wave_args]
    specs = [pl.BlockSpec((9, channels), lambda i: (0, 0)), halo_spec, halo_spec]
    specs += [above_spec, main_spec, below_spec] + wave_specs
    aliases = {}
    if prior is not None:
        aliases = {len(operands): 0}
        operands.append(prior)
        specs.append(pl.BlockSpec(memory_space=pl.ANY))
    kernel = make_epilogue_kernel(in_wave, offset, rows // block_rows - 1)
    return pl.pallas_call(
        kernel,
        grid=(count // block_rows,),
        in_specs=specs,
        out_specs=main_spec,
        out_shape=jax.ShapeDtypeStruct((rows, width, channels), jnp.bfloat16),
        input_output_aliases=aliases,
        compiler_params=pltpu.CompilerParams(dimension_semantics=("arbitrary",)),
    )(*operands)


def on_device(field, w_first, b_first, w_second, b_second, conv_kernel, mode_plan):
    rows, width, channels = field.shape
    lat_count = lax.axis_size("lat")
    lon_count = lax.axis_size("lon")
    devs = lat_count * lon_count
    per_device = KW // devs
    blocks = KH // MB
    slots = mode_plan.shape[0] // lat_count
    height = rows * devs
    me = lax.axis_index("lat") * lon_count + lax.axis_index("lon")
    n = devs * slots * 2
    chunks = 2 if rows % 8 == 0 else 1
    part = rows // chunks

    plan = mode_plan.reshape(lat_count, slots, lon_count).transpose(0, 2, 1).reshape(devs, slots)
    valid = plan >= 0
    tile = jnp.maximum(plan, 0)
    local_mode = tile // blocks
    lat_block = tile % blocks
    modes = jnp.arange(devs, dtype=jnp.int32)[:, None] * per_device + local_mode

    angles = lon_angles(modes.reshape(-1), width)
    factor = 1.0 / math.sqrt(width)
    lon_sub = (jnp.stack([jnp.cos(angles), -jnp.sin(angles)], axis=-1) * factor).astype(jnp.bfloat16)
    pencils = []
    if n <= 512:
        lon_t = jnp.transpose(lon_sub, (1, 2, 0)).reshape(n, width)
        for c in range(chunks):
            forward = forward_rows(field, lon_t, c * part, part)
            forward = forward.reshape(part, devs, slots, 2, channels)
            forward = jnp.transpose(forward, (1, 2, 3, 0, 4))
            pencils.append(
                lax.all_to_all(forward, ("lat", "lon"), split_axis=0, concat_axis=0, tiled=True)
            )
    else:
        values = field.astype(jnp.float32)
        average = jnp.mean(values, axis=-1, keepdims=True)
        centred = values - average
        spread = jnp.mean(centred * centred, axis=-1, keepdims=True)
        normed = (centred * lax.rsqrt(spread + 1e-05)).astype(jnp.bfloat16)
        forward = jnp.einsum("hwc,wna->nahc", normed, lon_sub, preferred_element_type=jnp.float32)
        forward = forward.astype(jnp.bfloat16).reshape(devs, slots, 2, rows, channels)
        chunks, part = 1, rows
        pencils.append(
            lax.all_to_all(forward, ("lat", "lon"), split_axis=0, concat_axis=0, tiled=True)
        )

    my_block = lax.dynamic_index_in_dim(lat_block, me, 0, keepdims=False)
    my_valid = lax.dynamic_index_in_dim(valid, me, 0, keepdims=False)
    my_mode = lax.dynamic_index_in_dim(local_mode, me, 0, keepdims=False)
    lat_modes = my_block[:, None] * MB + jnp.arange(MB, dtype=jnp.int32)[None, :]
    cosine, sine = lat_trig(lat_modes, height)
    lat_fwd = jnp.stack(
        [jnp.stack([cosine, sine], axis=2), jnp.stack([-sine, cosine], axis=2)], axis=1
    ).astype(jnp.bfloat16)
    lat_fwd = lat_fwd.reshape(slots, 2, MB, 2, devs, rows)
    spectrum = None
    for c in range(chunks):
        term = jnp.einsum(
            "joqasr,sjarc->jqoc",
            lat_fwd[..., c * part : (c + 1) * part],
            pencils[c],
            preferred_element_type=jnp.float32,
        )
        spectrum = term if spectrum is None else spectrum + term
    tiles = spectrum.astype(jnp.bfloat16).reshape(slots, MB, 2 * channels)

    first_mat = complexify(w_first)
    second_mat = complexify(w_second)
    shrunk = spectral_mlp(tiles, first_mat, b_first, second_mat, b_second)
    filtered = jnp.where(my_valid[:, None, None], shrunk, 0.0).astype(jnp.bfloat16)
    filtered = filtered.reshape(slots, MB, 2, channels)

    lat_inv = jnp.stack(
        [jnp.stack([cosine, -sine], axis=1), jnp.stack([sine, cosine], axis=1)], axis=1
    ).astype(jnp.bfloat16)
    lat_inv = lat_inv.reshape(slots, 2, 2, MB, devs, rows)
    same = (my_mode[:, None] == my_mode[None, :]) & my_valid[None, :]
    earlier = jnp.tril(jnp.ones((slots, slots), jnp.bool_), -1)
    first = my_valid & ~jnp.any(same & earlier, axis=1)
    merge = (same & first[:, None]).astype(jnp.float32)

    inv_angles = lon_angles(modes.reshape(-1), width)
    weights = jnp.where(modes.reshape(-1) == 0, 1.0, 2.0).astype(jnp.float32) / math.sqrt(width)
    lon_inv = jnp.stack(
        [weights * jnp.cos(inv_angles), -weights * jnp.sin(inv_angles)], axis=-1
    ).astype(jnp.bfloat16)
    lon_inv = lon_inv.reshape(width, n)

    forward_pairs = [(i, i + 1) for i in range(devs - 1)]
    backward_pairs = [(t, s) for s, t in forward_pairs]
    low = lax.ppermute(field[rows - 1 :], ("lat", "lon"), forward_pairs)
    high = lax.ppermute(field[:1], ("lat", "lon"), backward_pairs)

    partial = jnp.einsum(
        "jabqsr,jqbc->sjarc", lat_inv, filtered, preferred_element_type=jnp.float32
    )
    combined = jnp.einsum(
        "jk,skarc->sjarc", merge, partial, precision=lax.Precision.HIGHEST,
        preferred_element_type=jnp.float32,
    )
    inverse = combined.astype(jnp.bfloat16)
    rowwise = lax.all_to_all(inverse, ("lat", "lon"), split_axis=0, concat_axis=0, tiled=True)
    grid_rows = jnp.transpose(rowwise, (3, 0, 1, 2, 4)).reshape(rows, n, channels)
    if n <= 512:
        wave_args = (grid_rows, lon_inv)
    else:
        wave = jnp.einsum("rnc,wn->rwc", grid_rows, lon_inv, preferred_element_type=jnp.float32)
        wave_args = (wave.astype(jnp.bfloat16),)
    return epilogue(field, low, high, conv_kernel, wave_args, 0, rows, None)


def solution(mesh):
    placed = (P(("ens", "lat", "lon"), None, None), P(), P(), P(), P(), P(), P())
    return jax.shard_map(
        on_device,
        mesh=mesh,
        in_specs=placed,
        out_specs=P(("ens", "lat", "lon"), None, None),
        check_vma=False,
    )
```

```python
import math

import jax
import jax.numpy as jnp
from jax import lax
from jax.experimental import pallas as pl
from jax.experimental.pallas import tpu as pltpu
from jax.sharding import PartitionSpec as P

H = 1024
W = 1920
KH = 512
KW = 512
MB = 128


shrink_level = 0.01


def complexify(weights):
    real_part = weights[0]
    imag_part = weights[1]
    top_rows = jnp.concatenate([real_part, imag_part], axis=1)
    low_rows = jnp.concatenate([-imag_part, real_part], axis=1)
    return jnp.concatenate([top_rows, low_rows], axis=0)


def spectral_mlp(modes, first_mat, first_bias, second_mat, second_bias):
    hidden = jnp.einsum("tmc,cd->tmd", modes, first_mat, preferred_element_type=jnp.float32)
    hidden = jax.nn.relu(hidden + first_bias.reshape(-1)).astype(jnp.bfloat16)
    second_out = jnp.einsum("tmc,cd->tmd", hidden, second_mat, preferred_element_type=jnp.float32)
    second_out = second_out + second_bias.reshape(-1)
    return second_out - jnp.clip(second_out, -shrink_level, shrink_level)


def lon_angles(modes, width):
    columns = jnp.arange(width, dtype=jnp.int32)[:, None]
    phases = columns * modes[None, :] % width
    return phases.astype(jnp.float32) * (2.0 * math.pi / width)


def lat_trig(lat_modes, height, rowids=None):
    freqs = lat_modes - KH // 2
    if rowids is None:
        rowids = jnp.arange(height, dtype=jnp.int32)
    phases = jnp.mod(freqs[..., None] * rowids, height)
    angles = phases.astype(jnp.float32) * (2.0 * math.pi / height)
    factor = 1.0 / math.sqrt(height)
    return jnp.cos(angles) * factor, jnp.sin(angles) * factor


def forward_kernel(field_ref, lon_ref, out_ref):
    block_rows, _, channels = field_ref.shape
    lon = lon_ref[...]
    for h in range(block_rows):
        x = field_ref[h].astype(jnp.float32)
        average = jnp.sum(x, axis=1, keepdims=True) * (1.0 / channels)
        centred = x - average
        spread = jnp.sum(centred * centred, axis=1, keepdims=True) * (1.0 / channels)
        normed = (centred * lax.rsqrt(spread + 1e-05)).astype(jnp.bfloat16)
        out_ref[h] = jnp.dot(lon, normed, preferred_element_type=jnp.float32).astype(jnp.bfloat16)


def forward_rows(field, lon_t, start, count):
    _, width, channels = field.shape
    n = lon_t.shape[0]
    block_rows = math.gcd(count, 4)
    offset = start // block_rows
    return pl.pallas_call(
        forward_kernel,
        grid=(count // block_rows,),
        in_specs=[
            pl.BlockSpec((block_rows, width, channels), lambda i: (i + offset, 0, 0)),
            pl.BlockSpec((n, width), lambda i: (0, 0)),
        ],
        out_specs=pl.BlockSpec((block_rows, n, channels), lambda i: (i, 0, 0)),
        out_shape=jax.ShapeDtypeStruct((count, n, channels), jnp.bfloat16),
        compiler_params=pltpu.CompilerParams(dimension_semantics=("arbitrary",)),
    )(field, lon_t)


def make_epilogue_kernel(in_wave, first_block, last_block):
    def kernel(taps_ref, low_ref, high_ref, above_ref, main_ref, below_ref, *refs):
        out_ref = refs[-1]
        block_rows, width, _ = main_ref.shape
        step = pl.program_id(0) + first_block
        taps = [taps_ref[pl.ds(i, 1), :] for i in range(9)]
        first_row = jnp.where(step == 0, low_ref[0], above_ref[0]).astype(jnp.float32)
        last_row = jnp.where(step == last_block, high_ref[0], below_ref[0])
        last_row = last_row.astype(jnp.float32)

        def row(i):
            if i < 0:
                return first_row
            if i >= block_rows:
                return last_row
            return main_ref[i].astype(jnp.float32)

        for h in range(block_rows):
            xs = [row(h - 1), row(h), row(h + 1)]
            cols = [taps[s] * xs[0] + taps[3 + s] * xs[1] + taps[6 + s] * xs[2] for s in range(3)]
            stencil = pltpu.roll(cols[0], 1, 0) + cols[1] + pltpu.roll(cols[2], width - 1, 0)
            if in_wave:
                grid_ref, lon_ref = refs[0], refs[1]
                wave = jnp.dot(lon_ref[...], grid_ref[h], preferred_element_type=jnp.float32)
            else:
                wave = refs[0][h].astype(jnp.float32)
            out_ref[h] = ((xs[1] + wave) + stencil).astype(jnp.bfloat16)

    return kernel


def epilogue(field, low, high, conv_kernel, wave_args, start, count, prior):
    rows, width, channels = field.shape
    block_rows = math.gcd(count, 8)
    offset = start // block_rows
    taps = conv_kernel.reshape(9, channels)
    halo_spec = pl.BlockSpec((1, width, channels), lambda i: (0, 0, 0))
    above_spec = pl.BlockSpec(
        (1, width, channels), lambda i: (jnp.maximum((i + offset) * block_rows - 1, 0), 0, 0)
    )
    below_spec = pl.BlockSpec(
        (1, width, channels),
        lambda i: (jnp.minimum((i + offset + 1) * block_rows, rows - 1), 0, 0),
    )
    main_spec = pl.BlockSpec((block_rows, width, channels), lambda i: (i + offset, 0, 0))
    in_wave = len(wave_args) == 2
    if in_wave:
        grid_rows, lon_inv = wave_args
        n = grid_rows.shape[1]
        wave_specs = [
            pl.BlockSpec((block_rows, n, channels), lambda i: (i, 0, 0)),
            pl.BlockSpec((width, n), lambda i: (0, 0)),
        ]
    else:
        wave_specs = [pl.BlockSpec((block_rows, width, channels), lambda i: (i, 0, 0))]
    operands = [taps, low, high, field, field, field, *wave_args]
    specs = [pl.BlockSpec((9, channels), lambda i: (0, 0)), halo_spec, halo_spec]
    specs += [above_spec, main_spec, below_spec] + wave_specs
    aliases = {}
    if prior is not None:
        aliases = {len(operands): 0}
        operands.append(prior)
        specs.append(pl.BlockSpec(memory_space=pl.ANY))
    kernel = make_epilogue_kernel(in_wave, offset, rows // block_rows - 1)
    return pl.pallas_call(
        kernel,
        grid=(count // block_rows,),
        in_specs=specs,
        out_specs=main_spec,
        out_shape=jax.ShapeDtypeStruct((rows, width, channels), jnp.bfloat16),
        input_output_aliases=aliases,
        compiler_params=pltpu.CompilerParams(dimension_semantics=("arbitrary",)),
    )(*operands)


def on_device(field, w_first, b_first, w_second, b_second, conv_kernel, mode_plan):
    rows, width, channels = field.shape
    lat_count = lax.axis_size("lat")
    lon_count = lax.axis_size("lon")
    devs = lat_count * lon_count
    per_device = KW // devs
    blocks = KH // MB
    slots = mode_plan.shape[0] // lat_count
    height = rows * devs
    me = lax.axis_index("lat") * lon_count + lax.axis_index("lon")
    n = devs * slots * 2
    chunks = 2 if rows % 8 == 0 else 1
    part = rows // chunks

    plan = mode_plan.reshape(lat_count, slots, lon_count).transpose(0, 2, 1).reshape(devs, slots)
    valid = plan >= 0
    tile = jnp.maximum(plan, 0)
    local_mode = tile // blocks
    lat_block = tile % blocks
    modes = jnp.arange(devs, dtype=jnp.int32)[:, None] * per_device + local_mode

    angles = lon_angles(modes.reshape(-1), width)
    factor = 1.0 / math.sqrt(width)
    lon_sub = (jnp.stack([jnp.cos(angles), -jnp.sin(angles)], axis=-1) * factor).astype(jnp.bfloat16)
    pencils = []
    if n <= 512:
        lon_t = jnp.transpose(lon_sub, (1, 2, 0)).reshape(n, width)
        for c in range(chunks):
            forward = forward_rows(field, lon_t, c * part, part)
            forward = forward.reshape(part, devs, slots, 2, channels)
            forward = jnp.transpose(forward, (1, 2, 3, 0, 4))
            pencils.append(
                lax.all_to_all(forward, ("lat", "lon"), split_axis=0, concat_axis=0, tiled=True)
            )
    else:
        values = field.astype(jnp.float32)
        average = jnp.mean(values, axis=-1, keepdims=True)
        centred = values - average
        spread = jnp.mean(centred * centred, axis=-1, keepdims=True)
        normed = (centred * lax.rsqrt(spread + 1e-05)).astype(jnp.bfloat16)
        forward = jnp.einsum("hwc,wna->nahc", normed, lon_sub, preferred_element_type=jnp.float32)
        forward = forward.astype(jnp.bfloat16).reshape(devs, slots, 2, rows, channels)
        chunks, part = 1, rows
        pencils.append(
            lax.all_to_all(forward, ("lat", "lon"), split_axis=0, concat_axis=0, tiled=True)
        )

    my_block = lax.dynamic_index_in_dim(lat_block, me, 0, keepdims=False)
    my_valid = lax.dynamic_index_in_dim(valid, me, 0, keepdims=False)
    my_mode = lax.dynamic_index_in_dim(local_mode, me, 0, keepdims=False)
    lat_modes = my_block[:, None] * MB + jnp.arange(MB, dtype=jnp.int32)[None, :]
    cosine, sine = lat_trig(lat_modes, height)
    lat_fwd = jnp.stack(
        [jnp.stack([cosine, sine], axis=2), jnp.stack([-sine, cosine], axis=2)], axis=1
    ).astype(jnp.bfloat16)
    lat_fwd = lat_fwd.reshape(slots, 2, MB, 2, devs, rows)
    spectrum = None
    for c in range(chunks):
        term = jnp.einsum(
            "joqasr,sjarc->jqoc",
            lat_fwd[..., c * part : (c + 1) * part],
            pencils[c],
            preferred_element_type=jnp.float32,
        )
        spectrum = term if spectrum is None else spectrum + term
    tiles = spectrum.astype(jnp.bfloat16).reshape(slots, MB, 2 * channels)

    first_mat = complexify(w_first)
    second_mat = complexify(w_second)
    shrunk = spectral_mlp(tiles, first_mat, b_first, second_mat, b_second)
    filtered = jnp.where(my_valid[:, None, None], shrunk, 0.0).astype(jnp.bfloat16)
    filtered = filtered.reshape(slots, MB, 2, channels)

    inv_angles = lon_angles(modes.reshape(-1), width)
    weights = jnp.where(modes.reshape(-1) == 0, 1.0, 2.0).astype(jnp.float32) / math.sqrt(width)
    lon_inv = jnp.stack(
        [weights * jnp.cos(inv_angles), -weights * jnp.sin(inv_angles)], axis=-1
    ).astype(jnp.bfloat16)
    lon_inv = lon_inv.reshape(width, n)

    forward_pairs = [(i, i + 1) for i in range(devs - 1)]
    backward_pairs = [(t, s) for s, t in forward_pairs]
    low = lax.ppermute(field[rows - 1 :], ("lat", "lon"), forward_pairs)
    high = lax.ppermute(field[:1], ("lat", "lon"), backward_pairs)

    if n <= 512:
        gathered = lax.all_gather(filtered, ("lat", "lon"), axis=0, tiled=True)
        block_modes = (
            jnp.arange(blocks, dtype=jnp.int32)[:, None] * MB
            + jnp.arange(MB, dtype=jnp.int32)[None, :]
        )
        my_rows = me * rows + jnp.arange(rows, dtype=jnp.int32)
        row_cos, row_sin = lat_trig(block_modes, height, my_rows)
        inv_table = jnp.stack(
            [jnp.stack([row_cos, -row_sin], axis=1), jnp.stack([row_sin, row_cos], axis=1)],
            axis=1,
        ).astype(jnp.bfloat16)
        chosen = jnp.take(inv_table, lat_block.reshape(-1), axis=0)
        partial = jnp.einsum(
            "nabqr,nqbc->rnac", chosen, gathered, preferred_element_type=jnp.float32
        )
        partial = partial.reshape(rows, devs, slots, 2, channels)
        same_all = (local_mode[:, :, None] == local_mode[:, None, :]) & valid[:, None, :]
        earlier = jnp.tril(jnp.ones((slots, slots), jnp.bool_), -1)
        first_all = valid & ~jnp.any(same_all & earlier[None], axis=2)
        merge_all = (same_all & first_all[:, :, None]).astype(jnp.float32)
        combined = jnp.einsum(
            "djk,rdkac->rdjac", merge_all, partial, precision=lax.Precision.HIGHEST,
            preferred_element_type=jnp.float32,
        )
        grid_rows = combined.astype(jnp.bfloat16).reshape(rows, n, channels)
        wave_args = (grid_rows, lon_inv)
    else:
        lat_inv = jnp.stack(
            [jnp.stack([cosine, -sine], axis=1), jnp.stack([sine, cosine], axis=1)], axis=1
        ).astype(jnp.bfloat16)
        lat_inv = lat_inv.reshape(slots, 2, 2, MB, devs, rows)
        same = (my_mode[:, None] == my_mode[None, :]) & my_valid[None, :]
        earlier = jnp.tril(jnp.ones((slots, slots), jnp.bool_), -1)
        first = my_valid & ~jnp.any(same & earlier, axis=1)
        merge = (same & first[:, None]).astype(jnp.float32)

        partial = jnp.einsum(
            "jabqsr,jqbc->sjarc", lat_inv, filtered, preferred_element_type=jnp.float32
        )
        combined = jnp.einsum(
            "jk,skarc->sjarc", merge, partial, precision=lax.Precision.HIGHEST,
            preferred_element_type=jnp.float32,
        )
        inverse = combined.astype(jnp.bfloat16)
        rowwise = lax.all_to_all(inverse, ("lat", "lon"), split_axis=0, concat_axis=0, tiled=True)
        grid_rows = jnp.transpose(rowwise, (3, 0, 1, 2, 4)).reshape(rows, n, channels)
        wave = jnp.einsum("rnc,wn->rwc", grid_rows, lon_inv, preferred_element_type=jnp.float32)
        wave_args = (wave.astype(jnp.bfloat16),)
    return epilogue(field, low, high, conv_kernel, wave_args, 0, rows, None)


def solution(mesh):
    placed = (P(("ens", "lat", "lon"), None, None), P(), P(), P(), P(), P(), P())
    return jax.shard_map(
        on_device,
        mesh=mesh,
        in_specs=placed,
        out_specs=P(("ens", "lat", "lon"), None, None),
        check_vma=False,
    )
```

```python
import math

import jax
import jax.numpy as jnp
from jax import lax
from jax.experimental import pallas as pl
from jax.experimental.pallas import tpu as pltpu
from jax.sharding import PartitionSpec as P

H = 1024
W = 1920
KH = 512
KW = 512
MB = 128


shrink_level = 0.01


def complexify(weights):
    real_part = weights[0]
    imag_part = weights[1]
    top_rows = jnp.concatenate([real_part, imag_part], axis=1)
    low_rows = jnp.concatenate([-imag_part, real_part], axis=1)
    return jnp.concatenate([top_rows, low_rows], axis=0)


def spectral_mlp(modes, first_mat, first_bias, second_mat, second_bias):
    hidden = jnp.einsum("tmc,cd->tmd", modes, first_mat, preferred_element_type=jnp.float32)
    hidden = jax.nn.relu(hidden + first_bias.reshape(-1)).astype(jnp.bfloat16)
    second_out = jnp.einsum("tmc,cd->tmd", hidden, second_mat, preferred_element_type=jnp.float32)
    second_out = second_out + second_bias.reshape(-1)
    return second_out - jnp.clip(second_out, -shrink_level, shrink_level)


def lon_angles(modes, width):
    columns = jnp.arange(width, dtype=jnp.int32)[:, None]
    phases = columns * modes[None, :] % width
    return phases.astype(jnp.float32) * (2.0 * math.pi / width)


def lat_trig(lat_modes, height):
    freqs = lat_modes - KH // 2
    rowids = jnp.arange(height, dtype=jnp.int32)
    phases = jnp.mod(freqs[..., None] * rowids, height)
    angles = phases.astype(jnp.float32) * (2.0 * math.pi / height)
    factor = 1.0 / math.sqrt(height)
    return jnp.cos(angles) * factor, jnp.sin(angles) * factor


def forward_kernel(field_ref, lon_ref, out_ref):
    block_rows, _, channels = field_ref.shape
    lon = lon_ref[...]
    for h in range(block_rows):
        x = field_ref[h].astype(jnp.float32)
        average = jnp.sum(x, axis=1, keepdims=True) * (1.0 / channels)
        centred = x - average
        spread = jnp.sum(centred * centred, axis=1, keepdims=True) * (1.0 / channels)
        normed = (centred * lax.rsqrt(spread + 1e-05)).astype(jnp.bfloat16)
        out_ref[:, h, :] = jnp.dot(lon, normed, preferred_element_type=jnp.float32).astype(
            jnp.bfloat16
        )


def forward_rows(field, lon_t, start, count):
    _, width, channels = field.shape
    n = lon_t.shape[0]
    block_rows = math.gcd(count, 8)
    offset = start // block_rows
    return pl.pallas_call(
        forward_kernel,
        grid=(count // block_rows,),
        in_specs=[
            pl.BlockSpec((block_rows, width, channels), lambda i: (i + offset, 0, 0)),
            pl.BlockSpec((n, width), lambda i: (0, 0)),
        ],
        out_specs=pl.BlockSpec((n, block_rows, channels), lambda i: (0, i, 0)),
        out_shape=jax.ShapeDtypeStruct((n, count, channels), jnp.bfloat16),
        compiler_params=pltpu.CompilerParams(dimension_semantics=("arbitrary",)),
    )(field, lon_t)


def make_epilogue_kernel(in_wave, first_block, last_block):
    def kernel(taps_ref, low_ref, high_ref, above_ref, main_ref, below_ref, *refs):
        out_ref = refs[-1]
        block_rows, width, _ = main_ref.shape
        step = pl.program_id(0) + first_block
        taps = [taps_ref[pl.ds(i, 1), :] for i in range(9)]
        first_row = jnp.where(step == 0, low_ref[0], above_ref[0]).astype(jnp.float32)
        last_row = jnp.where(step == last_block, high_ref[0], below_ref[0])
        last_row = last_row.astype(jnp.float32)

        def row(i):
            if i < 0:
                return first_row
            if i >= block_rows:
                return last_row
            return main_ref[i].astype(jnp.float32)

        for h in range(block_rows):
            xs = [row(h - 1), row(h), row(h + 1)]
            cols = [taps[s] * xs[0] + taps[3 + s] * xs[1] + taps[6 + s] * xs[2] for s in range(3)]
            stencil = pltpu.roll(cols[0], 1, 0) + cols[1] + pltpu.roll(cols[2], width - 1, 0)
            if in_wave:
                grid_ref, lon_ref = refs[0], refs[1]
                wave = jnp.dot(lon_ref[...], grid_ref[h], preferred_element_type=jnp.float32)
            else:
                wave = refs[0][h].astype(jnp.float32)
            out_ref[h] = ((xs[1] + wave) + stencil).astype(jnp.bfloat16)

    return kernel


def epilogue(field, low, high, conv_kernel, wave_args, start, count, prior):
    rows, width, channels = field.shape
    block_rows = math.gcd(count, 8)
    offset = start // block_rows
    taps = conv_kernel.reshape(9, channels)
    halo_spec = pl.BlockSpec((1, width, channels), lambda i: (0, 0, 0))
    above_spec = pl.BlockSpec(
        (1, width, channels), lambda i: (jnp.maximum((i + offset) * block_rows - 1, 0), 0, 0)
    )
    below_spec = pl.BlockSpec(
        (1, width, channels),
        lambda i: (jnp.minimum((i + offset + 1) * block_rows, rows - 1), 0, 0),
    )
    main_spec = pl.BlockSpec((block_rows, width, channels), lambda i: (i + offset, 0, 0))
    in_wave = len(wave_args) == 2
    if in_wave:
        grid_rows, lon_inv = wave_args
        n = grid_rows.shape[1]
        wave_specs = [
            pl.BlockSpec((block_rows, n, channels), lambda i: (i, 0, 0)),
            pl.BlockSpec((width, n), lambda i: (0, 0)),
        ]
    else:
        wave_specs = [pl.BlockSpec((block_rows, width, channels), lambda i: (i, 0, 0))]
    operands = [taps, low, high, field, field, field, *wave_args]
    specs = [pl.BlockSpec((9, channels), lambda i: (0, 0)), halo_spec, halo_spec]
    specs += [above_spec, main_spec, below_spec] + wave_specs
    aliases = {}
    if prior is not None:
        aliases = {len(operands): 0}
        operands.append(prior)
        specs.append(pl.BlockSpec(memory_space=pl.ANY))
    kernel = make_epilogue_kernel(in_wave, offset, rows // block_rows - 1)
    return pl.pallas_call(
        kernel,
        grid=(count // block_rows,),
        in_specs=specs,
        out_specs=main_spec,
        out_shape=jax.ShapeDtypeStruct((rows, width, channels), jnp.bfloat16),
        input_output_aliases=aliases,
        compiler_params=pltpu.CompilerParams(dimension_semantics=("arbitrary",)),
    )(*operands)


def on_device(field, w_first, b_first, w_second, b_second, conv_kernel, mode_plan):
    rows, width, channels = field.shape
    lat_count = lax.axis_size("lat")
    lon_count = lax.axis_size("lon")
    devs = lat_count * lon_count
    per_device = KW // devs
    blocks = KH // MB
    slots = mode_plan.shape[0] // lat_count
    height = rows * devs
    me = lax.axis_index("lat") * lon_count + lax.axis_index("lon")
    n = devs * slots * 2
    chunks = 2 if rows % 8 == 0 else 1
    part = rows // chunks

    plan = mode_plan.reshape(lat_count, slots, lon_count).transpose(0, 2, 1).reshape(devs, slots)
    valid = plan >= 0
    tile = jnp.maximum(plan, 0)
    local_mode = tile // blocks
    lat_block = tile % blocks
    modes = jnp.arange(devs, dtype=jnp.int32)[:, None] * per_device + local_mode

    angles = lon_angles(modes.reshape(-1), width)
    factor = 1.0 / math.sqrt(width)
    lon_sub = (jnp.stack([jnp.cos(angles), -jnp.sin(angles)], axis=-1) * factor).astype(jnp.bfloat16)
    pencils = []
    if n <= 512:
        lon_t = jnp.transpose(lon_sub, (1, 2, 0)).reshape(n, width)
        for c in range(chunks):
            forward = forward_rows(field, lon_t, c * part, part)
            forward = forward.reshape(devs, slots, 2, part, channels)
            pencils.append(
                lax.all_to_all(forward, ("lat", "lon"), split_axis=0, concat_axis=0, tiled=True)
            )
    else:
        values = field.astype(jnp.float32)
        average = jnp.mean(values, axis=-1, keepdims=True)
        centred = values - average
        spread = jnp.mean(centred * centred, axis=-1, keepdims=True)
        normed = (centred * lax.rsqrt(spread + 1e-05)).astype(jnp.bfloat16)
        forward = jnp.einsum("hwc,wna->nahc", normed, lon_sub, preferred_element_type=jnp.float32)
        forward = forward.astype(jnp.bfloat16).reshape(devs, slots, 2, rows, channels)
        chunks, part = 1, rows
        pencils.append(
            lax.all_to_all(forward, ("lat", "lon"), split_axis=0, concat_axis=0, tiled=True)
        )

    my_block = lax.dynamic_index_in_dim(lat_block, me, 0, keepdims=False)
    my_valid = lax.dynamic_index_in_dim(valid, me, 0, keepdims=False)
    my_mode = lax.dynamic_index_in_dim(local_mode, me, 0, keepdims=False)
    lat_modes = my_block[:, None] * MB + jnp.arange(MB, dtype=jnp.int32)[None, :]
    cosine, sine = lat_trig(lat_modes, height)
    lat_fwd = jnp.stack(
        [jnp.stack([cosine, sine], axis=2), jnp.stack([-sine, cosine], axis=2)], axis=1
    ).astype(jnp.bfloat16)
    lat_fwd = lat_fwd.reshape(slots, 2, MB, 2, devs, rows)
    spectrum = None
    for c in range(chunks):
        term = jnp.einsum(
            "joqasr,sjarc->jqoc",
            lat_fwd[..., c * part : (c + 1) * part],
            pencils[c],
            preferred_element_type=jnp.float32,
        )
        spectrum = term if spectrum is None else spectrum + term
    tiles = spectrum.astype(jnp.bfloat16).reshape(slots, MB, 2 * channels)

    first_mat = complexify(w_first)
    second_mat = complexify(w_second)
    shrunk = spectral_mlp(tiles, first_mat, b_first, second_mat, b_second)
    filtered = jnp.where(my_valid[:, None, None], shrunk, 0.0).astype(jnp.bfloat16)
    filtered = filtered.reshape(slots, MB, 2, channels)

    lat_inv = jnp.stack(
        [jnp.stack([cosine, -sine], axis=1), jnp.stack([sine, cosine], axis=1)], axis=1
    ).astype(jnp.bfloat16)
    lat_inv = lat_inv.reshape(slots, 2, 2, MB, devs, rows)
    same = (my_mode[:, None] == my_mode[None, :]) & my_valid[None, :]
    earlier = jnp.tril(jnp.ones((slots, slots), jnp.bool_), -1)
    first = my_valid & ~jnp.any(same & earlier, axis=1)
    merge = (same & first[:, None]).astype(jnp.float32)

    inv_angles = lon_angles(modes.reshape(-1), width)
    weights = jnp.where(modes.reshape(-1) == 0, 1.0, 2.0).astype(jnp.float32) / math.sqrt(width)
    lon_inv = jnp.stack(
        [weights * jnp.cos(inv_angles), -weights * jnp.sin(inv_angles)], axis=-1
    ).astype(jnp.bfloat16)
    lon_inv = lon_inv.reshape(width, n)

    forward_pairs = [(i, i + 1) for i in range(devs - 1)]
    backward_pairs = [(t, s) for s, t in forward_pairs]
    low = lax.ppermute(field[rows - 1 :], ("lat", "lon"), forward_pairs)
    high = lax.ppermute(field[:1], ("lat", "lon"), backward_pairs)

    partial = jnp.einsum(
        "jabqsr,jqbc->sjarc", lat_inv, filtered, preferred_element_type=jnp.float32
    )
    combined = jnp.einsum(
        "jk,skarc->sjarc", merge, partial, precision=lax.Precision.HIGHEST,
        preferred_element_type=jnp.float32,
    )
    inverse = combined.astype(jnp.bfloat16)
    rowwise = lax.all_to_all(inverse, ("lat", "lon"), split_axis=0, concat_axis=0, tiled=True)
    grid_rows = jnp.transpose(rowwise, (3, 0, 1, 2, 4)).reshape(rows, n, channels)
    if n <= 512:
        wave_args = (grid_rows, lon_inv)
    else:
        wave = jnp.einsum("rnc,wn->rwc", grid_rows, lon_inv, preferred_element_type=jnp.float32)
        wave_args = (wave.astype(jnp.bfloat16),)
    return epilogue(field, low, high, conv_kernel, wave_args, 0, rows, None)


def solution(mesh):
    placed = (P(("ens", "lat", "lon"), None, None), P(), P(), P(), P(), P(), P())
    return jax.shard_map(
        on_device,
        mesh=mesh,
        in_specs=placed,
        out_specs=P(("ens", "lat", "lon"), None, None),
        check_vma=False,
    )
```

```python
import math

import jax
import jax.numpy as jnp
from jax import lax
from jax.experimental import pallas as pl
from jax.experimental.pallas import tpu as pltpu
from jax.sharding import PartitionSpec as P

H = 1024
W = 1920
KH = 512
KW = 512
MB = 128


shrink_level = 0.01


def complexify(weights):
    real_part = weights[0]
    imag_part = weights[1]
    top_rows = jnp.concatenate([real_part, imag_part], axis=1)
    low_rows = jnp.concatenate([-imag_part, real_part], axis=1)
    return jnp.concatenate([top_rows, low_rows], axis=0)


def spectral_mlp(modes, first_mat, first_bias, second_mat, second_bias):
    hidden = jnp.einsum("tmc,cd->tmd", modes, first_mat, preferred_element_type=jnp.float32)
    hidden = jax.nn.relu(hidden + first_bias.reshape(-1)).astype(jnp.bfloat16)
    second_out = jnp.einsum("tmc,cd->tmd", hidden, second_mat, preferred_element_type=jnp.float32)
    second_out = second_out + second_bias.reshape(-1)
    return second_out - jnp.clip(second_out, -shrink_level, shrink_level)


def lon_angles(modes, width):
    columns = jnp.arange(width, dtype=jnp.int32)[:, None]
    phases = columns * modes[None, :] % width
    return phases.astype(jnp.float32) * (2.0 * math.pi / width)


def lat_trig(lat_modes, height):
    freqs = lat_modes - KH // 2
    rowids = jnp.arange(height, dtype=jnp.int32)
    phases = jnp.mod(freqs[..., None] * rowids, height)
    angles = phases.astype(jnp.float32) * (2.0 * math.pi / height)
    factor = 1.0 / math.sqrt(height)
    return jnp.cos(angles) * factor, jnp.sin(angles) * factor


def forward_kernel(field_ref, lon_ref, out_ref):
    block_rows, _, channels = field_ref.shape
    lon = lon_ref[...]
    for h in range(block_rows):
        x = field_ref[h].astype(jnp.float32)
        average = jnp.sum(x, axis=1, keepdims=True) * (1.0 / channels)
        centred = x - average
        spread = jnp.sum(centred * centred, axis=1, keepdims=True) * (1.0 / channels)
        normed = (centred * lax.rsqrt(spread + 1e-05)).astype(jnp.bfloat16)
        out_ref[:, h, :] = jnp.dot(lon, normed, preferred_element_type=jnp.float32).astype(
            jnp.bfloat16
        )


def forward_rows(field, lon_t, start, count):
    _, width, channels = field.shape
    n = lon_t.shape[0]
    block_rows = math.gcd(count, 8)
    offset = start // block_rows
    return pl.pallas_call(
        forward_kernel,
        grid=(count // block_rows,),
        in_specs=[
            pl.BlockSpec((block_rows, width, channels), lambda i: (i + offset, 0, 0)),
            pl.BlockSpec((n, width), lambda i: (0, 0)),
        ],
        out_specs=pl.BlockSpec((n, block_rows, channels), lambda i: (0, i, 0)),
        out_shape=jax.ShapeDtypeStruct((n, count, channels), jnp.bfloat16),
        compiler_params=pltpu.CompilerParams(dimension_semantics=("arbitrary",)),
    )(field, lon_t)


def make_epilogue_kernel(in_wave, first_block, last_block):
    def kernel(taps_ref, low_ref, high_ref, above_ref, main_ref, below_ref, *refs):
        out_ref = refs[-1]
        block_rows, width, _ = main_ref.shape
        step = pl.program_id(0) + first_block
        taps = [taps_ref[pl.ds(i, 1), :] for i in range(9)]
        first_row = jnp.where(step == 0, low_ref[0], above_ref[0]).astype(jnp.float32)
        last_row = jnp.where(step == last_block, high_ref[0], below_ref[0])
        last_row = last_row.astype(jnp.float32)

        def row(i):
            if i < 0:
                return first_row
            if i >= block_rows:
                return last_row
            return main_ref[i].astype(jnp.float32)

        for h in range(block_rows):
            xs = [row(h - 1), row(h), row(h + 1)]
            cols = [taps[s] * xs[0] + taps[3 + s] * xs[1] + taps[6 + s] * xs[2] for s in range(3)]
            stencil = pltpu.roll(cols[0], 1, 0) + cols[1] + pltpu.roll(cols[2], width - 1, 0)
            if in_wave:
                grid_ref, lon_ref = refs[0], refs[1]
                wave = jnp.dot(lon_ref[...], grid_ref[:, h, :], preferred_element_type=jnp.float32)
            else:
                wave = refs[0][h].astype(jnp.float32)
            out_ref[h] = ((xs[1] + wave) + stencil).astype(jnp.bfloat16)

    return kernel


def epilogue(field, low, high, conv_kernel, wave_args, start, count, prior):
    rows, width, channels = field.shape
    block_rows = math.gcd(count, 8)
    offset = start // block_rows
    taps = conv_kernel.reshape(9, channels)
    halo_spec = pl.BlockSpec((1, width, channels), lambda i: (0, 0, 0))
    above_spec = pl.BlockSpec(
        (1, width, channels), lambda i: (jnp.maximum((i + offset) * block_rows - 1, 0), 0, 0)
    )
    below_spec = pl.BlockSpec(
        (1, width, channels),
        lambda i: (jnp.minimum((i + offset + 1) * block_rows, rows - 1), 0, 0),
    )
    main_spec = pl.BlockSpec((block_rows, width, channels), lambda i: (i + offset, 0, 0))
    in_wave = len(wave_args) == 2
    if in_wave:
        grid_rows, lon_inv = wave_args
        n = grid_rows.shape[0]
        wave_specs = [
            pl.BlockSpec((n, block_rows, channels), lambda i: (0, i, 0)),
            pl.BlockSpec((width, n), lambda i: (0, 0)),
        ]
    else:
        wave_specs = [pl.BlockSpec((block_rows, width, channels), lambda i: (i, 0, 0))]
    operands = [taps, low, high, field, field, field, *wave_args]
    specs = [pl.BlockSpec((9, channels), lambda i: (0, 0)), halo_spec, halo_spec]
    specs += [above_spec, main_spec, below_spec] + wave_specs
    aliases = {}
    if prior is not None:
        aliases = {len(operands): 0}
        operands.append(prior)
        specs.append(pl.BlockSpec(memory_space=pl.ANY))
    kernel = make_epilogue_kernel(in_wave, offset, rows // block_rows - 1)
    return pl.pallas_call(
        kernel,
        grid=(count // block_rows,),
        in_specs=specs,
        out_specs=main_spec,
        out_shape=jax.ShapeDtypeStruct((rows, width, channels), jnp.bfloat16),
        input_output_aliases=aliases,
        compiler_params=pltpu.CompilerParams(dimension_semantics=("arbitrary",)),
    )(*operands)


def on_device(field, w_first, b_first, w_second, b_second, conv_kernel, mode_plan):
    rows, width, channels = field.shape
    lat_count = lax.axis_size("lat")
    lon_count = lax.axis_size("lon")
    devs = lat_count * lon_count
    per_device = KW // devs
    blocks = KH // MB
    slots = mode_plan.shape[0] // lat_count
    height = rows * devs
    me = lax.axis_index("lat") * lon_count + lax.axis_index("lon")
    n = devs * slots * 2
    chunks = 2 if rows % 8 == 0 else 1
    part = rows // chunks

    plan = mode_plan.reshape(lat_count, slots, lon_count).transpose(0, 2, 1).reshape(devs, slots)
    valid = plan >= 0
    tile = jnp.maximum(plan, 0)
    local_mode = tile // blocks
    lat_block = tile % blocks
    modes = jnp.arange(devs, dtype=jnp.int32)[:, None] * per_device + local_mode

    angles = lon_angles(modes.reshape(-1), width)
    factor = 1.0 / math.sqrt(width)
    lon_sub = (jnp.stack([jnp.cos(angles), -jnp.sin(angles)], axis=-1) * factor).astype(jnp.bfloat16)
    pencils = []
    if n <= 512:
        lon_t = jnp.transpose(lon_sub, (1, 2, 0)).reshape(n, width)
        for c in range(chunks):
            forward = forward_rows(field, lon_t, c * part, part)
            forward = forward.reshape(devs, slots, 2, part, channels)
            pencils.append(
                lax.all_to_all(forward, ("lat", "lon"), split_axis=0, concat_axis=0, tiled=True)
            )
    else:
        values = field.astype(jnp.float32)
        average = jnp.mean(values, axis=-1, keepdims=True)
        centred = values - average
        spread = jnp.mean(centred * centred, axis=-1, keepdims=True)
        normed = (centred * lax.rsqrt(spread + 1e-05)).astype(jnp.bfloat16)
        forward = jnp.einsum("hwc,wna->nahc", normed, lon_sub, preferred_element_type=jnp.float32)
        forward = forward.astype(jnp.bfloat16).reshape(devs, slots, 2, rows, channels)
        chunks, part = 1, rows
        pencils.append(
            lax.all_to_all(forward, ("lat", "lon"), split_axis=0, concat_axis=0, tiled=True)
        )

    my_block = lax.dynamic_index_in_dim(lat_block, me, 0, keepdims=False)
    my_valid = lax.dynamic_index_in_dim(valid, me, 0, keepdims=False)
    my_mode = lax.dynamic_index_in_dim(local_mode, me, 0, keepdims=False)
    lat_modes = my_block[:, None] * MB + jnp.arange(MB, dtype=jnp.int32)[None, :]
    cosine, sine = lat_trig(lat_modes, height)
    lat_fwd = jnp.stack(
        [jnp.stack([cosine, sine], axis=2), jnp.stack([-sine, cosine], axis=2)], axis=1
    ).astype(jnp.bfloat16)
    lat_fwd = lat_fwd.reshape(slots, 2, MB, 2, devs, rows)
    spectrum = None
    for c in range(chunks):
        term = jnp.einsum(
            "joqasr,sjarc->jqoc",
            lat_fwd[..., c * part : (c + 1) * part],
            pencils[c],
            preferred_element_type=jnp.float32,
        )
        spectrum = term if spectrum is None else spectrum + term
    tiles = spectrum.astype(jnp.bfloat16).reshape(slots, MB, 2 * channels)

    first_mat = complexify(w_first)
    second_mat = complexify(w_second)
    shrunk = spectral_mlp(tiles, first_mat, b_first, second_mat, b_second)
    filtered = jnp.where(my_valid[:, None, None], shrunk, 0.0).astype(jnp.bfloat16)
    filtered = filtered.reshape(slots, MB, 2, channels)

    lat_inv = jnp.stack(
        [jnp.stack([cosine, -sine], axis=1), jnp.stack([sine, cosine], axis=1)], axis=1
    ).astype(jnp.bfloat16)
    lat_inv = lat_inv.reshape(slots, 2, 2, MB, devs, rows)
    same = (my_mode[:, None] == my_mode[None, :]) & my_valid[None, :]
    earlier = jnp.tril(jnp.ones((slots, slots), jnp.bool_), -1)
    first = my_valid & ~jnp.any(same & earlier, axis=1)
    merge = (same & first[:, None]).astype(jnp.float32)

    inv_angles = lon_angles(modes.reshape(-1), width)
    weights = jnp.where(modes.reshape(-1) == 0, 1.0, 2.0).astype(jnp.float32) / math.sqrt(width)
    lon_inv = jnp.stack(
        [weights * jnp.cos(inv_angles), -weights * jnp.sin(inv_angles)], axis=-1
    ).astype(jnp.bfloat16)
    lon_inv = lon_inv.reshape(width, n)

    forward_pairs = [(i, i + 1) for i in range(devs - 1)]
    backward_pairs = [(t, s) for s, t in forward_pairs]
    low = lax.ppermute(field[rows - 1 :], ("lat", "lon"), forward_pairs)
    high = lax.ppermute(field[:1], ("lat", "lon"), backward_pairs)

    partial = jnp.einsum(
        "jabqsr,jqbc->sjarc", lat_inv, filtered, preferred_element_type=jnp.float32
    )
    combined = jnp.einsum(
        "jk,skarc->sjarc", merge, partial, precision=lax.Precision.HIGHEST,
        preferred_element_type=jnp.float32,
    )
    inverse = combined.astype(jnp.bfloat16)
    rowwise = lax.all_to_all(inverse, ("lat", "lon"), split_axis=0, concat_axis=0, tiled=True)
    if n <= 512:
        wave_args = (rowwise.reshape(n, rows, channels), lon_inv)
    else:
        grid_rows = jnp.transpose(rowwise, (3, 0, 1, 2, 4)).reshape(rows, n, channels)
        wave = jnp.einsum("rnc,wn->rwc", grid_rows, lon_inv, preferred_element_type=jnp.float32)
        wave_args = (wave.astype(jnp.bfloat16),)
    return epilogue(field, low, high, conv_kernel, wave_args, 0, rows, None)


def solution(mesh):
    placed = (P(("ens", "lat", "lon"), None, None), P(), P(), P(), P(), P(), P())
    return jax.shard_map(
        on_device,
        mesh=mesh,
        in_specs=placed,
        out_specs=P(("ens", "lat", "lon"), None, None),
        check_vma=False,
    )
```

```python
import math

import jax
import jax.numpy as jnp
from jax import lax
from jax.experimental import pallas as pl
from jax.experimental.pallas import tpu as pltpu
from jax.sharding import PartitionSpec as P

H = 1024
W = 1920
KH = 512
KW = 512
MB = 128


shrink_level = 0.01


def complexify(weights):
    real_part = weights[0]
    imag_part = weights[1]
    top_rows = jnp.concatenate([real_part, imag_part], axis=1)
    low_rows = jnp.concatenate([-imag_part, real_part], axis=1)
    return jnp.concatenate([top_rows, low_rows], axis=0)


def spectral_mlp(modes, first_mat, first_bias, second_mat, second_bias):
    hidden = jnp.einsum("tmc,cd->tmd", modes, first_mat, preferred_element_type=jnp.float32)
    hidden = jax.nn.relu(hidden + first_bias.reshape(-1)).astype(jnp.bfloat16)
    second_out = jnp.einsum("tmc,cd->tmd", hidden, second_mat, preferred_element_type=jnp.float32)
    second_out = second_out + second_bias.reshape(-1)
    return second_out - jnp.clip(second_out, -shrink_level, shrink_level)


def lon_angles(modes, width):
    columns = jnp.arange(width, dtype=jnp.int32)[:, None]
    phases = columns * modes[None, :] % width
    return phases.astype(jnp.float32) * (2.0 * math.pi / width)


def lat_trig(lat_modes, height):
    freqs = lat_modes - KH // 2
    rowids = jnp.arange(height, dtype=jnp.int32)
    phases = jnp.mod(freqs[..., None] * rowids, height)
    angles = phases.astype(jnp.float32) * (2.0 * math.pi / height)
    factor = 1.0 / math.sqrt(height)
    return jnp.cos(angles) * factor, jnp.sin(angles) * factor


def forward_kernel(field_ref, lon_ref, out_ref):
    block_rows, _, channels = field_ref.shape
    lon = lon_ref[...]
    for h in range(block_rows):
        x = field_ref[h].astype(jnp.float32)
        average = jnp.sum(x, axis=1, keepdims=True) * (1.0 / channels)
        centred = x - average
        spread = jnp.sum(centred * centred, axis=1, keepdims=True) * (1.0 / channels)
        normed = (centred * lax.rsqrt(spread + 1e-05)).astype(jnp.bfloat16)
        out_ref[:, h, :] = jnp.dot(lon, normed, preferred_element_type=jnp.float32).astype(
            jnp.bfloat16
        )


def forward_rows(field, lon_t, start, count):
    _, width, channels = field.shape
    n = lon_t.shape[0]
    block_rows = math.gcd(count, 8)
    offset = start // block_rows
    return pl.pallas_call(
        forward_kernel,
        grid=(count // block_rows,),
        in_specs=[
            pl.BlockSpec((block_rows, width, channels), lambda i: (i + offset, 0, 0)),
            pl.BlockSpec((n, width), lambda i: (0, 0)),
        ],
        out_specs=pl.BlockSpec((n, block_rows, channels), lambda i: (0, i, 0)),
        out_shape=jax.ShapeDtypeStruct((n, count, channels), jnp.bfloat16),
        compiler_params=pltpu.CompilerParams(dimension_semantics=("arbitrary",)),
    )(field, lon_t)


def make_epilogue_kernel(in_wave, first_block, last_block):
    def kernel(taps_ref, low_ref, high_ref, above_ref, main_ref, below_ref, *refs):
        out_ref = refs[-1]
        block_rows, width, _ = main_ref.shape
        step = pl.program_id(0) + first_block
        taps = [taps_ref[pl.ds(i, 1), :] for i in range(9)]
        taps[4] = taps[4] + 1.0
        first_row = jnp.where(step == 0, low_ref[0], above_ref[0]).astype(jnp.float32)
        last_row = jnp.where(step == last_block, high_ref[0], below_ref[0])
        last_row = last_row.astype(jnp.float32)

        def row(i):
            if i < 0:
                return first_row
            if i >= block_rows:
                return last_row
            return main_ref[i].astype(jnp.float32)

        for h in range(block_rows):
            xs = [row(h - 1), row(h), row(h + 1)]
            cols = [taps[s] * xs[0] + taps[3 + s] * xs[1] + taps[6 + s] * xs[2] for s in range(3)]
            stencil = pltpu.roll(cols[0], 1, 0) + cols[1] + pltpu.roll(cols[2], width - 1, 0)
            if in_wave:
                grid_ref, lon_ref = refs[0], refs[1]
                wave = jnp.dot(lon_ref[...], grid_ref[h], preferred_element_type=jnp.float32)
            else:
                wave = refs[0][h].astype(jnp.float32)
            out_ref[h] = (stencil + wave).astype(jnp.bfloat16)

    return kernel


def epilogue(field, low, high, conv_kernel, wave_args, start, count, prior):
    rows, width, channels = field.shape
    block_rows = math.gcd(count, 8)
    offset = start // block_rows
    taps = conv_kernel.reshape(9, channels)
    halo_spec = pl.BlockSpec((1, width, channels), lambda i: (0, 0, 0))
    above_spec = pl.BlockSpec(
        (1, width, channels), lambda i: (jnp.maximum((i + offset) * block_rows - 1, 0), 0, 0)
    )
    below_spec = pl.BlockSpec(
        (1, width, channels),
        lambda i: (jnp.minimum((i + offset + 1) * block_rows, rows - 1), 0, 0),
    )
    main_spec = pl.BlockSpec((block_rows, width, channels), lambda i: (i + offset, 0, 0))
    in_wave = len(wave_args) == 2
    if in_wave:
        grid_rows, lon_inv = wave_args
        n = grid_rows.shape[1]
        wave_specs = [
            pl.BlockSpec((block_rows, n, channels), lambda i: (i, 0, 0)),
            pl.BlockSpec((width, n), lambda i: (0, 0)),
        ]
    else:
        wave_specs = [pl.BlockSpec((block_rows, width, channels), lambda i: (i, 0, 0))]
    operands = [taps, low, high, field, field, field, *wave_args]
    specs = [pl.BlockSpec((9, channels), lambda i: (0, 0)), halo_spec, halo_spec]
    specs += [above_spec, main_spec, below_spec] + wave_specs
    aliases = {}
    if prior is not None:
        aliases = {len(operands): 0}
        operands.append(prior)
        specs.append(pl.BlockSpec(memory_space=pl.ANY))
    kernel = make_epilogue_kernel(in_wave, offset, rows // block_rows - 1)
    return pl.pallas_call(
        kernel,
        grid=(count // block_rows,),
        in_specs=specs,
        out_specs=main_spec,
        out_shape=jax.ShapeDtypeStruct((rows, width, channels), jnp.bfloat16),
        input_output_aliases=aliases,
        compiler_params=pltpu.CompilerParams(dimension_semantics=("arbitrary",)),
    )(*operands)


def on_device(field, w_first, b_first, w_second, b_second, conv_kernel, mode_plan):
    rows, width, channels = field.shape
    lat_count = lax.axis_size("lat")
    lon_count = lax.axis_size("lon")
    devs = lat_count * lon_count
    per_device = KW // devs
    blocks = KH // MB
    slots = mode_plan.shape[0] // lat_count
    height = rows * devs
    me = lax.axis_index("lat") * lon_count + lax.axis_index("lon")
    n = devs * slots * 2
    chunks = 2 if rows % 8 == 0 else 1
    part = rows // chunks

    plan = mode_plan.reshape(lat_count, slots, lon_count).transpose(0, 2, 1).reshape(devs, slots)
    valid = plan >= 0
    tile = jnp.maximum(plan, 0)
    local_mode = tile // blocks
    lat_block = tile % blocks
    modes = jnp.arange(devs, dtype=jnp.int32)[:, None] * per_device + local_mode

    angles = lon_angles(modes.reshape(-1), width)
    factor = 1.0 / math.sqrt(width)
    lon_sub = (jnp.stack([jnp.cos(angles), -jnp.sin(angles)], axis=-1) * factor).astype(jnp.bfloat16)
    pencils = []
    if n <= 512:
        lon_t = jnp.transpose(lon_sub, (1, 2, 0)).reshape(n, width)
        for c in range(chunks):
            forward = forward_rows(field, lon_t, c * part, part)
            forward = forward.reshape(devs, slots, 2, part, channels)
            pencils.append(
                lax.all_to_all(forward, ("lat", "lon"), split_axis=0, concat_axis=0, tiled=True)
            )
    else:
        values = field.astype(jnp.float32)
        average = jnp.mean(values, axis=-1, keepdims=True)
        centred = values - average
        spread = jnp.mean(centred * centred, axis=-1, keepdims=True)
        normed = (centred * lax.rsqrt(spread + 1e-05)).astype(jnp.bfloat16)
        forward = jnp.einsum("hwc,wna->nahc", normed, lon_sub, preferred_element_type=jnp.float32)
        forward = forward.astype(jnp.bfloat16).reshape(devs, slots, 2, rows, channels)
        chunks, part = 1, rows
        pencils.append(
            lax.all_to_all(forward, ("lat", "lon"), split_axis=0, concat_axis=0, tiled=True)
        )

    my_block = lax.dynamic_index_in_dim(lat_block, me, 0, keepdims=False)
    my_valid = lax.dynamic_index_in_dim(valid, me, 0, keepdims=False)
    my_mode = lax.dynamic_index_in_dim(local_mode, me, 0, keepdims=False)
    lat_modes = my_block[:, None] * MB + jnp.arange(MB, dtype=jnp.int32)[None, :]
    cosine, sine = lat_trig(lat_modes, height)
    lat_fwd = jnp.stack(
        [jnp.stack([cosine, sine], axis=2), jnp.stack([-sine, cosine], axis=2)], axis=1
    ).astype(jnp.bfloat16)
    lat_fwd = lat_fwd.reshape(slots, 2, MB, 2, devs, rows)
    spectrum = None
    for c in range(chunks):
        term = jnp.einsum(
            "joqasr,sjarc->jqoc",
            lat_fwd[..., c * part : (c + 1) * part],
            pencils[c],
            preferred_element_type=jnp.float32,
        )
        spectrum = term if spectrum is None else spectrum + term
    tiles = spectrum.astype(jnp.bfloat16).reshape(slots, MB, 2 * channels)

    first_mat = complexify(w_first)
    second_mat = complexify(w_second)
    shrunk = spectral_mlp(tiles, first_mat, b_first, second_mat, b_second)
    filtered = jnp.where(my_valid[:, None, None], shrunk, 0.0).astype(jnp.bfloat16)
    filtered = filtered.reshape(slots, MB, 2, channels)

    lat_inv = jnp.stack(
        [jnp.stack([cosine, -sine], axis=1), jnp.stack([sine, cosine], axis=1)], axis=1
    ).astype(jnp.bfloat16)
    lat_inv = lat_inv.reshape(slots, 2, 2, MB, devs, rows)
    same = (my_mode[:, None] == my_mode[None, :]) & my_valid[None, :]
    earlier = jnp.tril(jnp.ones((slots, slots), jnp.bool_), -1)
    first = my_valid & ~jnp.any(same & earlier, axis=1)
    merge = (same & first[:, None]).astype(jnp.float32)

    inv_angles = lon_angles(modes.reshape(-1), width)
    weights = jnp.where(modes.reshape(-1) == 0, 1.0, 2.0).astype(jnp.float32) / math.sqrt(width)
    lon_inv = jnp.stack(
        [weights * jnp.cos(inv_angles), -weights * jnp.sin(inv_angles)], axis=-1
    ).astype(jnp.bfloat16)
    lon_inv = lon_inv.reshape(width, n)

    forward_pairs = [(i, i + 1) for i in range(devs - 1)]
    backward_pairs = [(t, s) for s, t in forward_pairs]
    low = lax.ppermute(field[rows - 1 :], ("lat", "lon"), forward_pairs)
    high = lax.ppermute(field[:1], ("lat", "lon"), backward_pairs)

    partial = jnp.einsum(
        "jabqsr,jqbc->sjarc", lat_inv, filtered, preferred_element_type=jnp.float32
    )
    combined = jnp.einsum(
        "jk,skarc->sjarc", merge, partial, precision=lax.Precision.HIGHEST,
        preferred_element_type=jnp.float32,
    )
    inverse = combined.astype(jnp.bfloat16)
    rowwise = lax.all_to_all(inverse, ("lat", "lon"), split_axis=0, concat_axis=0, tiled=True)
    grid_rows = jnp.transpose(rowwise, (3, 0, 1, 2, 4)).reshape(rows, n, channels)
    if n <= 512:
        wave_args = (grid_rows, lon_inv)
    else:
        wave = jnp.einsum("rnc,wn->rwc", grid_rows, lon_inv, preferred_element_type=jnp.float32)
        wave_args = (wave.astype(jnp.bfloat16),)
    return epilogue(field, low, high, conv_kernel, wave_args, 0, rows, None)


def solution(mesh):
    placed = (P(("ens", "lat", "lon"), None, None), P(), P(), P(), P(), P(), P())
    return jax.shard_map(
        on_device,
        mesh=mesh,
        in_specs=placed,
        out_specs=P(("ens", "lat", "lon"), None, None),
        check_vma=False,
    )
```

```python
import math

import jax
import jax.numpy as jnp
from jax import lax
from jax.experimental import pallas as pl
from jax.experimental.pallas import tpu as pltpu
from jax.sharding import PartitionSpec as P

H = 1024
W = 1920
KH = 512
KW = 512
MB = 128


shrink_level = 0.01


def complexify(weights):
    real_part = weights[0]
    imag_part = weights[1]
    top_rows = jnp.concatenate([real_part, imag_part], axis=1)
    low_rows = jnp.concatenate([-imag_part, real_part], axis=1)
    return jnp.concatenate([top_rows, low_rows], axis=0)


def spectral_mlp(modes, first_mat, first_bias, second_mat, second_bias):
    hidden = jnp.einsum("tmc,cd->tmd", modes, first_mat, preferred_element_type=jnp.float32)
    hidden = jax.nn.relu(hidden + first_bias.reshape(-1)).astype(jnp.bfloat16)
    second_out = jnp.einsum("tmc,cd->tmd", hidden, second_mat, preferred_element_type=jnp.float32)
    second_out = second_out + second_bias.reshape(-1)
    return second_out - jnp.clip(second_out, -shrink_level, shrink_level)


def lon_angles(modes, width):
    columns = jnp.arange(width, dtype=jnp.int32)[:, None]
    phases = columns * modes[None, :] % width
    return phases.astype(jnp.float32) * (2.0 * math.pi / width)


def lat_trig(lat_modes, height):
    freqs = lat_modes - KH // 2
    rowids = jnp.arange(height, dtype=jnp.int32)
    phases = jnp.mod(freqs[..., None] * rowids, height)
    angles = phases.astype(jnp.float32) * (2.0 * math.pi / height)
    factor = 1.0 / math.sqrt(height)
    return jnp.cos(angles) * factor, jnp.sin(angles) * factor


def forward_kernel(field_ref, lon_ref, out_ref):
    block_rows, _, channels = field_ref.shape
    lon = lon_ref[...]
    for h in range(block_rows):
        x = field_ref[h].astype(jnp.float32)
        average = jnp.sum(x, axis=1, keepdims=True) * (1.0 / channels)
        centred = x - average
        spread = jnp.sum(centred * centred, axis=1, keepdims=True) * (1.0 / channels)
        normed = (centred * lax.rsqrt(spread + 1e-05)).astype(jnp.bfloat16)
        out_ref[:, h, :] = jnp.dot(lon, normed, preferred_element_type=jnp.float32).astype(
            jnp.bfloat16
        )


def forward_rows(field, lon_t, start, count):
    _, width, channels = field.shape
    n = lon_t.shape[0]
    block_rows = math.gcd(count, 16)
    offset = start // block_rows
    return pl.pallas_call(
        forward_kernel,
        grid=(count // block_rows,),
        in_specs=[
            pl.BlockSpec((block_rows, width, channels), lambda i: (i + offset, 0, 0)),
            pl.BlockSpec((n, width), lambda i: (0, 0)),
        ],
        out_specs=pl.BlockSpec((n, block_rows, channels), lambda i: (0, i, 0)),
        out_shape=jax.ShapeDtypeStruct((n, count, channels), jnp.bfloat16),
        compiler_params=pltpu.CompilerParams(dimension_semantics=("arbitrary",)),
    )(field, lon_t)


def make_epilogue_kernel(in_wave, first_block, last_block):
    def kernel(taps_ref, low_ref, high_ref, above_ref, main_ref, below_ref, *refs):
        out_ref = refs[-1]
        block_rows, width, _ = main_ref.shape
        step = pl.program_id(0) + first_block
        taps = [taps_ref[pl.ds(i, 1), :] for i in range(9)]
        taps[4] = taps[4] + 1.0
        first_row = jnp.where(step == 0, low_ref[0], above_ref[0]).astype(jnp.float32)
        last_row = jnp.where(step == last_block, high_ref[0], below_ref[0])
        last_row = last_row.astype(jnp.float32)

        def row(i):
            if i < 0:
                return first_row
            if i >= block_rows:
                return last_row
            return main_ref[i].astype(jnp.float32)

        for h in range(block_rows):
            xs = [row(h - 1), row(h), row(h + 1)]
            cols = [taps[s] * xs[0] + taps[3 + s] * xs[1] + taps[6 + s] * xs[2] for s in range(3)]
            stencil = pltpu.roll(cols[0], 1, 0) + cols[1] + pltpu.roll(cols[2], width - 1, 0)
            if in_wave:
                grid_ref, lon_ref = refs[0], refs[1]
                wave = jnp.dot(lon_ref[...], grid_ref[h], preferred_element_type=jnp.float32)
            else:
                wave = refs[0][h].astype(jnp.float32)
            out_ref[h] = (stencil + wave).astype(jnp.bfloat16)

    return kernel


def epilogue(field, low, high, conv_kernel, wave_args, start, count, prior):
    rows, width, channels = field.shape
    block_rows = math.gcd(count, 8)
    offset = start // block_rows
    taps = conv_kernel.reshape(9, channels)
    halo_spec = pl.BlockSpec((1, width, channels), lambda i: (0, 0, 0))
    above_spec = pl.BlockSpec(
        (1, width, channels), lambda i: (jnp.maximum((i + offset) * block_rows - 1, 0), 0, 0)
    )
    below_spec = pl.BlockSpec(
        (1, width, channels),
        lambda i: (jnp.minimum((i + offset + 1) * block_rows, rows - 1), 0, 0),
    )
    main_spec = pl.BlockSpec((block_rows, width, channels), lambda i: (i + offset, 0, 0))
    in_wave = len(wave_args) == 2
    if in_wave:
        grid_rows, lon_inv = wave_args
        n = grid_rows.shape[1]
        wave_specs = [
            pl.BlockSpec((block_rows, n, channels), lambda i: (i, 0, 0)),
            pl.BlockSpec((width, n), lambda i: (0, 0)),
        ]
    else:
        wave_specs = [pl.BlockSpec((block_rows, width, channels), lambda i: (i, 0, 0))]
    operands = [taps, low, high, field, field, field, *wave_args]
    specs = [pl.BlockSpec((9, channels), lambda i: (0, 0)), halo_spec, halo_spec]
    specs += [above_spec, main_spec, below_spec] + wave_specs
    aliases = {}
    if prior is not None:
        aliases = {len(operands): 0}
        operands.append(prior)
        specs.append(pl.BlockSpec(memory_space=pl.ANY))
    kernel = make_epilogue_kernel(in_wave, offset, rows // block_rows - 1)
    return pl.pallas_call(
        kernel,
        grid=(count // block_rows,),
        in_specs=specs,
        out_specs=main_spec,
        out_shape=jax.ShapeDtypeStruct((rows, width, channels), jnp.bfloat16),
        input_output_aliases=aliases,
        compiler_params=pltpu.CompilerParams(dimension_semantics=("arbitrary",)),
    )(*operands)


def on_device(field, w_first, b_first, w_second, b_second, conv_kernel, mode_plan):
    rows, width, channels = field.shape
    lat_count = lax.axis_size("lat")
    lon_count = lax.axis_size("lon")
    devs = lat_count * lon_count
    per_device = KW // devs
    blocks = KH // MB
    slots = mode_plan.shape[0] // lat_count
    height = rows * devs
    me = lax.axis_index("lat") * lon_count + lax.axis_index("lon")
    n = devs * slots * 2
    chunks = 2 if rows % 8 == 0 else 1
    part = rows // chunks

    plan = mode_plan.reshape(lat_count, slots, lon_count).transpose(0, 2, 1).reshape(devs, slots)
    valid = plan >= 0
    tile = jnp.maximum(plan, 0)
    local_mode = tile // blocks
    lat_block = tile % blocks
    modes = jnp.arange(devs, dtype=jnp.int32)[:, None] * per_device + local_mode

    angles = lon_angles(modes.reshape(-1), width)
    factor = 1.0 / math.sqrt(width)
    lon_sub = (jnp.stack([jnp.cos(angles), -jnp.sin(angles)], axis=-1) * factor).astype(jnp.bfloat16)
    pencils = []
    if n <= 512:
        lon_t = jnp.transpose(lon_sub, (1, 2, 0)).reshape(n, width)
        for c in range(chunks):
            forward = forward_rows(field, lon_t, c * part, part)
            forward = forward.reshape(devs, slots, 2, part, channels)
            pencils.append(
                lax.all_to_all(forward, ("lat", "lon"), split_axis=0, concat_axis=0, tiled=True)
            )
    else:
        values = field.astype(jnp.float32)
        average = jnp.mean(values, axis=-1, keepdims=True)
        centred = values - average
        spread = jnp.mean(centred * centred, axis=-1, keepdims=True)
        normed = (centred * lax.rsqrt(spread + 1e-05)).astype(jnp.bfloat16)
        forward = jnp.einsum("hwc,wna->nahc", normed, lon_sub, preferred_element_type=jnp.float32)
        forward = forward.astype(jnp.bfloat16).reshape(devs, slots, 2, rows, channels)
        chunks, part = 1, rows
        pencils.append(
            lax.all_to_all(forward, ("lat", "lon"), split_axis=0, concat_axis=0, tiled=True)
        )

    my_block = lax.dynamic_index_in_dim(lat_block, me, 0, keepdims=False)
    my_valid = lax.dynamic_index_in_dim(valid, me, 0, keepdims=False)
    my_mode = lax.dynamic_index_in_dim(local_mode, me, 0, keepdims=False)
    lat_modes = my_block[:, None] * MB + jnp.arange(MB, dtype=jnp.int32)[None, :]
    cosine, sine = lat_trig(lat_modes, height)
    lat_fwd = jnp.stack(
        [jnp.stack([cosine, sine], axis=2), jnp.stack([-sine, cosine], axis=2)], axis=1
    ).astype(jnp.bfloat16)
    lat_fwd = lat_fwd.reshape(slots, 2, MB, 2, devs, rows)
    spectrum = None
    for c in range(chunks):
        term = jnp.einsum(
            "joqasr,sjarc->jqoc",
            lat_fwd[..., c * part : (c + 1) * part],
            pencils[c],
            preferred_element_type=jnp.float32,
        )
        spectrum = term if spectrum is None else spectrum + term
    tiles = spectrum.astype(jnp.bfloat16).reshape(slots, MB, 2 * channels)

    first_mat = complexify(w_first)
    second_mat = complexify(w_second)
    shrunk = spectral_mlp(tiles, first_mat, b_first, second_mat, b_second)
    filtered = jnp.where(my_valid[:, None, None], shrunk, 0.0).astype(jnp.bfloat16)
    filtered = filtered.reshape(slots, MB, 2, channels)

    lat_inv = jnp.stack(
        [jnp.stack([cosine, -sine], axis=1), jnp.stack([sine, cosine], axis=1)], axis=1
    ).astype(jnp.bfloat16)
    lat_inv = lat_inv.reshape(slots, 2, 2, MB, devs, rows)
    same = (my_mode[:, None] == my_mode[None, :]) & my_valid[None, :]
    earlier = jnp.tril(jnp.ones((slots, slots), jnp.bool_), -1)
    first = my_valid & ~jnp.any(same & earlier, axis=1)
    merge = (same & first[:, None]).astype(jnp.float32)

    inv_angles = lon_angles(modes.reshape(-1), width)
    weights = jnp.where(modes.reshape(-1) == 0, 1.0, 2.0).astype(jnp.float32) / math.sqrt(width)
    lon_inv = jnp.stack(
        [weights * jnp.cos(inv_angles), -weights * jnp.sin(inv_angles)], axis=-1
    ).astype(jnp.bfloat16)
    lon_inv = lon_inv.reshape(width, n)

    forward_pairs = [(i, i + 1) for i in range(devs - 1)]
    backward_pairs = [(t, s) for s, t in forward_pairs]
    low = lax.ppermute(field[rows - 1 :], ("lat", "lon"), forward_pairs)
    high = lax.ppermute(field[:1], ("lat", "lon"), backward_pairs)

    partial = jnp.einsum(
        "jabqsr,jqbc->sjarc", lat_inv, filtered, preferred_element_type=jnp.float32
    )
    combined = jnp.einsum(
        "jk,skarc->sjarc", merge, partial, precision=lax.Precision.HIGHEST,
        preferred_element_type=jnp.float32,
    )
    inverse = combined.astype(jnp.bfloat16)
    rowwise = lax.all_to_all(inverse, ("lat", "lon"), split_axis=0, concat_axis=0, tiled=True)
    grid_rows = jnp.transpose(rowwise, (3, 0, 1, 2, 4)).reshape(rows, n, channels)
    if n <= 512:
        wave_args = (grid_rows, lon_inv)
    else:
        wave = jnp.einsum("rnc,wn->rwc", grid_rows, lon_inv, preferred_element_type=jnp.float32)
        wave_args = (wave.astype(jnp.bfloat16),)
    return epilogue(field, low, high, conv_kernel, wave_args, 0, rows, None)


def solution(mesh):
    placed = (P(("ens", "lat", "lon"), None, None), P(), P(), P(), P(), P(), P())
    return jax.shard_map(
        on_device,
        mesh=mesh,
        in_specs=placed,
        out_specs=P(("ens", "lat", "lon"), None, None),
        check_vma=False,
    )
```
